128 devices in a mesh: seq: 16 (over y, x), head: 8 (over z, core).
Axes of the slice: x: 4, y: 4, z: 4, core: 2. Of those that a mesh axis runs over, the one named last changes fastest.
Arguments:
- spectra: bfloat16 [16, 8192, 1024], P('head', 'seq'), may hold values from -6 to 6
- key_bias: float32 [16, 8192], replicated, may hold values from -6 to 330
- valid_bins: int32 [16], replicated, may hold values from 128 to 8192, as said below
- enc_query: bfloat16 [1024, 1024], replicated, may hold values from -0.1875 to 0.1875
- enc_key: bfloat16 [1024, 1024], replicated, may hold values from -0.1875 to 0.1875
- enc_value: bfloat16 [1024, 1024], replicated, may hold values from -0.1875 to 0.1875
- enc_out: bfloat16 [1024, 1024], replicated, may hold values from -1.5 to 1.5
- token_ids: int32 [16, 512], P(None, 'seq'), may hold values from 0 to 27
- embedding: bfloat16 [28, 4096], replicated, may hold values from -6 to 6
- dec_query: bfloat16 [4096, 4096], P(None, 'head'), may hold values from -0.09375 to 0.09375
- mem_key: bfloat16 [1024, 4096], P(None, 'head'), may hold values from -0.1875 to 0.1875
- mem_value: bfloat16 [1024, 4096], P(None, 'head'), may hold values from -0.1875 to 0.1875
- dec_out: bfloat16 [4096, 4096], P('head'), may hold values from -0.5 to 0.5
Outputs:
- encoded: bfloat16 [16, 8192, 1024], P('head', 'seq')
- decoded: bfloat16 [16, 512, 4096], P(None, 'seq', 'head')
The draws below stay inside these ranges and needn't reach their ends.
Inputs may be any that keep to these rules, and one draw needn't show every extreme that they name: `valid_bins`: each count is a multiple of 128; bins from the count on are padding.
All inputs are finite; a program needn't handle non-finite values.
Results may differ from the reference program's by a relative error of at most 0.018.
Values may be sent and summed in bfloat16 or wider, within the bound.
No kernel may reach another device: no remote copies, remote signals or barrier semaphores. Data moves between devices by JAX's collectives and lax.ppermute only.
A program may use at most 192 MiB of HBM per device.

```python
import jax
import jax.numpy as jnp
from jax import lax

DM = 1024
HE = 16
HDE = 64
WINDOW = 512
POOL = 32
VBLOCK = 128
DD = 4096
HD = 32
HDD = 128
VOCAB = 28
DLEN = 512
BIN_DEV = 512
SPEC = 16
BINS = 8192


def draw_valid_bins(key, part):
    key_first, key_second = jax.random.split(jax.random.fold_in(key, 11))
    most_blocks = BINS // VBLOCK
    blocks = jax.random.randint(key_first, (SPEC,), 1, most_blocks + 1)
    ranking = jax.random.permutation(key_second, SPEC)
    blocks = jnp.where(ranking == 0, most_blocks, blocks)
    blocks = jnp.where(ranking == 1, 1, blocks)
    return (blocks * VBLOCK).astype(jnp.int32)


def draw_key_bias(key, part):
    key_base = jax.random.fold_in(jax.random.fold_in(key, 23), 0)
    return jnp.clip(1.5 * jax.random.normal(key_base, (SPEC, BINS), jnp.float32), -6.0, 6.0)


def touch_ends(entries, stream_key, smallest, top_value):
    longest = entries.shape.index(max(entries.shape))
    spots = []
    for shift in (0, 1):
        where = [jax.random.randint(jax.random.fold_in(stream_key, axis), (), 0, length) for axis, length in enumerate(entries.shape)]
        where[longest] = (where[longest] + shift) % entries.shape[longest]
        spots.append(tuple(where))
    return entries.at[spots[0]].set(smallest).at[spots[1]].set(top_value)


def spiked(result, stream_key, source, target, blocks, factor):
    owner, partner = [(jnp.arange(result.shape[axis_at]) // (result.shape[axis_at] // blocks)).reshape([-1 if axis == axis_at else 1 for axis in range(result.ndim)]) for axis_at in (source, target)]
    chosen = jax.random.permutation(stream_key, blocks)[partner]
    strong = (owner == chosen) | (owner == (partner + blocks // 2) % blocks)
    return jnp.where(strong, factor * result, result)


def level_of(key, extent, cuts, low, high):
    def one(position, parts):
        draws = jax.random.uniform(jax.random.fold_in(jax.random.fold_in(key, 6), position), (parts,), jnp.float32, low / len(cuts), high / len(cuts))
        return jnp.repeat(jnp.exp(draws), extent[position] // parts).reshape((-1,) + (1,) * (len(extent) - position - 1))

    gain = one(*cuts[0])
    for cut in cuts[1:]:
        gain = gain * one(*cut)
    return gain


def bell_draw(rng, shape, deviation, most, cuts=(), kind=jnp.bfloat16):
    entries = jax.random.normal(rng, shape, jnp.float32) * deviation
    if len(cuts) > 0:
        entries = level_of(rng, shape, cuts, -0.22, 0.18) * entries
    return jnp.clip(entries, min=-most, max=most).astype(kind)


def noise_with(rng, extent, width, most, shards, heavy, kind=jnp.bfloat16):
    drawn = width * jax.random.normal(rng, extent, jnp.float32)
    if shards:
        drawn = drawn * level_of(rng, extent, shards, -0.22, 0.18)
    return jnp.clip(spiked(drawn, jax.random.fold_in(rng, 3), *heavy), -most, most).astype(kind)


def setup_inputs(seed: int = 0) -> dict:
    keys = jax.random.split(jax.random.key(seed), 14)
    spectra = bell_draw(keys[0], (SPEC, BINS, DM), 1.0, 6.0, ((0, 8), (1, 16)))
    key_bias = draw_key_bias(jax.random.fold_in(keys[13], 71), 0)
    valid_bins = draw_valid_bins(jax.random.fold_in(keys[13], 71), 0)
    enc_query = bell_draw(keys[3], (DM, DM), DM ** -0.5, 0.1875)
    enc_key = bell_draw(keys[4], (DM, DM), DM ** -0.5, 0.1875)
    enc_value = bell_draw(keys[5], (DM, DM), DM ** -0.5, 0.1875)
    enc_out = bell_draw(keys[6], (DM, DM), (DM // 64) ** -0.5, 1.5)
    token_ids = touch_ends(jax.random.randint(keys[7], (SPEC, DLEN), 0, VOCAB), jax.random.fold_in(keys[7], 1), 0, VOCAB - 1).astype(jnp.int32)
    embedding = bell_draw(keys[8], (VOCAB, DD), 1.0, 6.0)
    dec_query = bell_draw(keys[9], (DD, DD), DD ** -0.5, 0.09375, ((1, 8),))
    mem_key = bell_draw(keys[10], (DM, DD), DM ** -0.5, 0.1875, ((1, 8),))
    mem_value = bell_draw(keys[11], (DM, DD), DM ** -0.5, 0.1875, ((1, 8),))
    dec_out = noise_with(keys[12], (DD, DD), (DD // 16) ** -0.5, 0.5, ((0, 8),), (0, 1, 8, 2.0))
    return dict(spectra=spectra, key_bias=key_bias, valid_bins=valid_bins, enc_query=enc_query, enc_key=enc_key, enc_value=enc_value, enc_out=enc_out, token_ids=token_ids, embedding=embedding, dec_query=dec_query, mem_key=mem_key, mem_value=mem_value, dec_out=dec_out)


epsilon = 1e-05
masked_score = -1e+30

def rms_rows(values_in):
    widened = values_in.astype(jnp.float32)
    inverse_rms = lax.rsqrt(lax.optimization_barrier(jnp.mean(widened * widened, axis=-1, keepdims=True)) + epsilon)
    return (widened * inverse_rms).astype(jnp.bfloat16)

def softmax_rows(scores):
    row_top = lax.optimization_barrier(jnp.max(scores, axis=-1, keepdims=True))
    weights = jnp.exp(scores - row_top)
    return (weights / lax.optimization_barrier(jnp.sum(weights, axis=-1, keepdims=True))).astype(jnp.bfloat16)

def encode_one(spectrum, bias_row, count_one, enc_query, kv_weights, enc_out):
    half_span = WINDOW // 2
    key_span = BIN_DEV + 2 * half_span
    normed = rms_rows(spectrum)
    query_enc = jnp.dot(normed, enc_query, preferred_element_type=jnp.float32).astype(jnp.bfloat16)
    keyval = jnp.dot(normed, kv_weights, preferred_element_type=jnp.float32).astype(jnp.bfloat16)
    padded = jnp.pad(keyval, ((half_span, half_span), (0, 0)))
    bias_pad = jnp.pad(bias_row, (half_span, half_span))

    def one_block(block_index):
        start_row = block_index * BIN_DEV
        q_block = lax.dynamic_slice_in_dim(query_enc, start_row, BIN_DEV, 0).reshape(BIN_DEV, HE, HDE).astype(jnp.float32)
        kv_block = lax.dynamic_slice_in_dim(padded, start_row, key_span, 0)
        bias_block = lax.dynamic_slice_in_dim(bias_pad, start_row, key_span, 0)
        key_heads = kv_block[:, :DM].reshape(key_span, HE, HDE).astype(jnp.float32)
        value_heads = kv_block[:, DM:].reshape(key_span, HE, HDE).astype(jnp.float32)
        scores = jnp.einsum('qhd,khd->hqk', q_block, key_heads) * HDE ** (-0.5) + bias_block[None, None, :]
        query_rows = start_row + jnp.arange(BIN_DEV, dtype=jnp.int32)
        key_cols = start_row - half_span + jnp.arange(key_span, dtype=jnp.int32)
        allowed = (jnp.abs(key_cols[None, :] - query_rows[:, None]) <= half_span) & (key_cols[None, :] >= 0) & (key_cols[None, :] < count_one)
        scores = jnp.where(allowed[None], scores, masked_score)
        weights = softmax_rows(scores).astype(jnp.float32)
        context = jnp.einsum('hqk,khd->qhd', weights, value_heads).astype(jnp.bfloat16)
        return context.reshape(BIN_DEV, DM)
    context = lax.map(one_block, jnp.arange(BINS // BIN_DEV, dtype=jnp.int32)).reshape(BINS, DM)
    attended = jnp.dot(context, enc_out, preferred_element_type=jnp.float32)
    valid_rows = (jnp.arange(BINS, dtype=jnp.int32) < count_one)[:, None]
    return jnp.where(valid_rows, spectrum.astype(jnp.float32) + attended, 0.0).astype(jnp.bfloat16)

def reference(spectra, key_bias, valid_bins, enc_query, enc_key, enc_value, enc_out, token_ids, embedding, dec_query, mem_key, mem_value, dec_out):
    kv_weights = jnp.concatenate([enc_key, enc_value], axis=1)

    def encode_spectrum(operands):
        spectrum, bias_row, count_one = operands
        return encode_one(spectrum, bias_row, count_one, enc_query, kv_weights, enc_out)
    encoded = lax.map(encode_spectrum, (spectra, key_bias, valid_bins))
    mem_len = BINS // POOL
    pooled = lax.optimization_barrier(jnp.mean(encoded.astype(jnp.float32).reshape(SPEC, mem_len, POOL, DM), axis=2)).astype(jnp.bfloat16)
    mem_normed = rms_rows(pooled).reshape(SPEC * mem_len, DM)
    key_mem = jnp.dot(mem_normed, mem_key, preferred_element_type=jnp.float32).astype(jnp.bfloat16).reshape(SPEC, mem_len, HD, HDD)
    value_mem = jnp.dot(mem_normed, mem_value, preferred_element_type=jnp.float32).astype(jnp.bfloat16).reshape(SPEC, mem_len, HD, HDD)
    pooled_bias = lax.optimization_barrier(jnp.max(key_bias.reshape(SPEC, mem_len, POOL), axis=2))
    mem_valid = jnp.arange(mem_len, dtype=jnp.int32)[None, :] * POOL < valid_bins[:, None]
    hidden = embedding[token_ids]
    normed_tok = rms_rows(hidden).reshape(SPEC * DLEN, DD)
    query_dec = jnp.dot(normed_tok, dec_query, preferred_element_type=jnp.float32).astype(jnp.bfloat16).reshape(SPEC, DLEN, HD, HDD)

    def cross_one(operands):
        q_one, k_one, v_one, bias_one, valid_one = operands
        scores = jnp.einsum('thd,phd->htp', q_one.astype(jnp.float32), k_one.astype(jnp.float32)) * HDD ** (-0.5) + bias_one[None, None, :]
        scores = jnp.where(valid_one[None, None, :], scores, masked_score)
        weights = softmax_rows(scores).astype(jnp.float32)
        context = jnp.einsum('htp,phd->thd', weights, v_one.astype(jnp.float32)).astype(jnp.bfloat16)
        return context.reshape(DLEN, DD)
    context = lax.map(cross_one, (query_dec, key_mem, value_mem, pooled_bias, mem_valid))
    attended = jnp.dot(context.reshape(SPEC * DLEN, DD), dec_out, preferred_element_type=jnp.float32).reshape(SPEC, DLEN, DD)
    decoded = (hidden.astype(jnp.float32) + attended).astype(jnp.bfloat16)
    return (encoded, decoded)
```

```python
import jax
import jax.numpy as jnp
from jax import lax
from jax.experimental import pallas as pl
from jax.experimental.pallas import tpu as pltpu
from jax.sharding import PartitionSpec as P

HE = 16
WINDOW = 512
POOL = 32
HD = 32
QBLOCK = 128
HGROUP = 512


epsilon = 1e-05
masked_score = -1e30


def rms_rows(values_in):
    widened = values_in.astype(jnp.float32)
    inverse_rms = lax.rsqrt(jnp.mean(widened * widened, axis=-1, keepdims=True) + epsilon)
    return (widened * inverse_rms).astype(jnp.bfloat16)


def softmax_rows(scores):
    row_top = jnp.max(scores, axis=-1, keepdims=True)
    weights = jnp.exp(scores - row_top)
    return (weights / jnp.sum(weights, axis=-1, keepdims=True)).astype(jnp.bfloat16)


def band_kernel(q_ref, k_ref, v_ref, b_ref, o_ref):
    qb = pl.program_id(2)
    q0 = pl.multiple_of(qb * QBLOCK, QBLOCK)
    kwin = QBLOCK + WINDOW
    bias = b_ref[0, 0]
    lane = lax.broadcasted_iota(jnp.int32, (1, 128), 1)
    low = lane < 64
    for pair in range(HGROUP // 128):
        cols = slice(pair * 128, (pair + 1) * 128)
        q = q_ref[0, :, cols] * 0.125
        k = k_ref[0, pl.ds(q0, kwin), cols]
        v = v_ref[0, pl.ds(q0, kwin), cols]
        out = None
        for half in range(2):
            sel = low if half == 0 else jnp.logical_not(low)
            qh = jnp.where(sel, q, jnp.zeros_like(q))
            s = lax.dot_general(
                qh, k, (((1,), (1,)), ((), ())), preferred_element_type=jnp.float32
            ) + bias
            m = jnp.max(s, axis=1, keepdims=True)
            p = jnp.exp(s - m)
            total = jnp.sum(p, axis=1, keepdims=True)
            pv = jnp.dot(p.astype(jnp.bfloat16), v, preferred_element_type=jnp.float32)
            pv = pv / total
            out = pv if out is None else jnp.where(low, out, pv)
        o_ref[0, :, cols] = out.astype(o_ref.dtype)


def band_attention(query_enc, keyval, full_bias):
    spec_dev, bin_dev, width = query_enc.shape
    key_span = keyval.shape[1]
    groups = width // HGROUP
    qblocks = bin_dev // QBLOCK
    kwin = QBLOCK + WINDOW
    return pl.pallas_call(
        band_kernel,
        out_shape=jax.ShapeDtypeStruct(query_enc.shape, jnp.bfloat16),
        grid=(spec_dev, groups, qblocks),
        in_specs=[
            pl.BlockSpec((1, QBLOCK, HGROUP), lambda s, g, b: (s, b, g)),
            pl.BlockSpec((1, key_span, HGROUP), lambda s, g, b: (s, 0, g)),
            pl.BlockSpec((1, key_span, HGROUP), lambda s, g, b: (s, 0, groups + g)),
            pl.BlockSpec((1, 1, QBLOCK, kwin), lambda s, g, b: (s, b, 0, 0)),
        ],
        out_specs=pl.BlockSpec((1, QBLOCK, HGROUP), lambda s, g, b: (s, b, g)),
        compiler_params=pltpu.CompilerParams(
            dimension_semantics=("arbitrary", "arbitrary", "arbitrary")
        ),
        cost_estimate=pl.CostEstimate(
            flops=spec_dev * bin_dev * kwin * width * 8,
            transcendentals=spec_dev * bin_dev * kwin * HE,
            bytes_accessed=spec_dev * (bin_dev * width * 4 + key_span * width * 4)
            + full_bias.size * 4,
        ),
    )(query_enc, keyval, keyval, full_bias)


def per_device(
    spectra,
    key_bias,
    valid_bins,
    enc_query,
    enc_key,
    enc_value,
    enc_out,
    token_ids,
    embedding,
    dec_query,
    mem_key,
    mem_value,
    dec_out,
):
    seq_pos = lax.axis_index("seq")
    head_pos = lax.axis_index("head")
    spec_dev, bin_dev, model_width = spectra.shape
    half_span = WINDOW // 2
    first_spec = head_pos * spec_dev
    first_bin = seq_pos * bin_dev
    my_counts = lax.dynamic_slice_in_dim(valid_bins, first_spec, spec_dev, 0)
    bias_pad = jnp.pad(key_bias, ((0, 0), (half_span, half_span)))
    my_bias = lax.dynamic_slice(
        bias_pad, (first_spec, first_bin), (spec_dev, bin_dev + 2 * half_span)
    )
    kv_weights = jnp.concatenate([enc_key, enc_value], axis=1)

    count = lax.axis_size("seq")
    forward = [(i, i + 1) for i in range(count - 1)]
    backward = [(target, source) for source, target in forward]
    low_edge = lax.ppermute(spectra[:, bin_dev - half_span :], "seq", forward)
    high_edge = lax.ppermute(spectra[:, :half_span], "seq", backward)

    normed = rms_rows(spectra)
    query_enc = jnp.einsum(
        "sbd,de->sbe", normed, enc_query, preferred_element_type=jnp.float32
    ).astype(jnp.bfloat16)
    keyval_mid = jnp.einsum(
        "sbd,de->sbe", normed, kv_weights, preferred_element_type=jnp.float32
    ).astype(jnp.bfloat16)
    edges = rms_rows(jnp.concatenate([low_edge, high_edge], axis=1))
    keyval_edges = jnp.einsum(
        "sbd,de->sbe", edges, kv_weights, preferred_element_type=jnp.float32
    ).astype(jnp.bfloat16)
    keyval = jnp.concatenate(
        [keyval_edges[:, :half_span], keyval_mid, keyval_edges[:, half_span:]], axis=1
    )
    key_span = bin_dev + 2 * half_span
    kwin = QBLOCK + WINDOW
    key_cols = first_bin - half_span + jnp.arange(key_span, dtype=jnp.int32)
    col_ok = (key_cols[None, :] >= 0) & (key_cols[None, :] < my_counts[:, None])
    col_bias = jnp.where(col_ok, my_bias, masked_score)
    windows = jnp.stack(
        [col_bias[:, b * QBLOCK : b * QBLOCK + kwin] for b in range(bin_dev // QBLOCK)], axis=1
    )
    offset = (
        jnp.arange(kwin, dtype=jnp.int32)[None, :] - jnp.arange(QBLOCK, dtype=jnp.int32)[:, None]
    )
    band = (offset >= 0) & (offset <= WINDOW)
    full_bias = jnp.where(band[None, None], windows[:, :, None, :], masked_score)
    context = band_attention(query_enc, keyval, full_bias)

    query_rows = first_bin + jnp.arange(bin_dev, dtype=jnp.int32)
    attended = jnp.einsum("sbd,de->sbe", context, enc_out, preferred_element_type=jnp.float32)
    valid_rows = (query_rows[None, :] < my_counts[:, None])[:, :, None]
    encoded = jnp.where(valid_rows, spectra.astype(jnp.float32) + attended, 0.0).astype(
        jnp.bfloat16
    )
    pooled = jnp.mean(
        encoded.astype(jnp.float32).reshape(spec_dev, bin_dev // POOL, POOL, model_width), axis=2
    ).astype(jnp.bfloat16)
    spectra_all = lax.all_gather(pooled, "head", axis=0, tiled=True)
    mem_weights = jnp.concatenate([mem_key, mem_value], axis=1)
    local_width = mem_key.shape[1]
    memory = lax.all_gather(
        jnp.einsum(
            "spd,de->spe", rms_rows(spectra_all), mem_weights, preferred_element_type=jnp.float32
        ).astype(jnp.bfloat16),
        "seq",
        axis=1,
        tiled=True,
    )
    spec_count = memory.shape[0]
    mem_len = memory.shape[1]
    pooled_bias = jnp.max(key_bias.reshape(spec_count, mem_len, POOL), axis=2)
    mem_valid = jnp.arange(mem_len, dtype=jnp.int32)[None, :] * POOL < valid_bins[:, None]
    tok_count = token_ids.shape[1]
    dec_width = embedding.shape[1]
    dec_head = dec_width // HD
    heads_here = local_width // dec_head
    onehot = (
        token_ids[:, :, None] == jnp.arange(embedding.shape[0], dtype=jnp.int32)[None, None, :]
    ).astype(jnp.bfloat16)
    hidden = jnp.einsum(
        "stv,vd->std", onehot, embedding, preferred_element_type=jnp.float32
    ).astype(jnp.bfloat16)
    normed_tok = rms_rows(hidden)
    query_dec = jnp.einsum(
        "std,de->ste", normed_tok, dec_query, preferred_element_type=jnp.float32
    ).astype(jnp.bfloat16)
    query_heads = query_dec.reshape(spec_count, tok_count, heads_here, dec_head)
    key_heads = memory[:, :, :local_width].reshape(spec_count, mem_len, heads_here, dec_head)
    value_heads = memory[:, :, local_width:].reshape(spec_count, mem_len, heads_here, dec_head)
    scores = (
        jnp.einsum("sthd,sphd->shtp", query_heads, key_heads, preferred_element_type=jnp.float32)
        * dec_head ** (-0.5)
        + pooled_bias[:, None, None, :]
    )
    scores = jnp.where(mem_valid[:, None, None, :], scores, masked_score)
    weights = softmax_rows(scores)
    dec_context = jnp.einsum(
        "shtp,sphd->sthd", weights, value_heads, preferred_element_type=jnp.float32
    ).astype(jnp.bfloat16)
    dec_context = dec_context.reshape(spec_count, tok_count, local_width)
    share_width = dec_width // lax.axis_size("head")
    partial_sums = jnp.einsum(
        "ste,ed->std", dec_context, dec_out, preferred_element_type=jnp.float32
    )
    summed = lax.psum_scatter(
        partial_sums.astype(jnp.bfloat16), "head", scatter_dimension=2, tiled=True
    ).astype(jnp.float32)
    own_part = lax.dynamic_slice_in_dim(hidden, head_pos * share_width, share_width, 2)
    decoded = (own_part.astype(jnp.float32) + summed).astype(jnp.bfloat16)
    return (encoded, decoded)


def solution(mesh):
    return jax.shard_map(
        per_device,
        mesh=mesh,
        in_specs=(
            P("head", "seq", None),
            P(),
            P(),
            P(),
            P(),
            P(),
            P(),
            P(None, "seq"),
            P(),
            P(None, "head"),
            P(None, "head"),
            P(None, "head"),
            P("head", None),
        ),
        out_specs=(P("head", "seq", None), P(None, "seq", "head")),
        check_vma=False,
    )
```

```python
import jax
import jax.numpy as jnp
from jax import lax
from jax.experimental import pallas as pl
from jax.experimental.pallas import tpu as pltpu
from jax.sharding import PartitionSpec as P

HE = 16
WINDOW = 512
POOL = 32
HD = 32
QBLOCK = 128
HGROUP = 512


epsilon = 1e-05
masked_score = -1e30


def rms_rows(values_in):
    widened = values_in.astype(jnp.float32)
    inverse_rms = lax.rsqrt(jnp.mean(widened * widened, axis=-1, keepdims=True) + epsilon)
    return (widened * inverse_rms).astype(jnp.bfloat16)


def softmax_rows(scores):
    row_top = jnp.max(scores, axis=-1, keepdims=True)
    weights = jnp.exp(scores - row_top)
    return (weights / jnp.sum(weights, axis=-1, keepdims=True)).astype(jnp.bfloat16)


def band_kernel(q_ref, k_ref, v_ref, b_ref, o_ref):
    qb = pl.program_id(2)
    q0 = pl.multiple_of(qb * QBLOCK, QBLOCK)
    kwin = QBLOCK + WINDOW
    bias = b_ref[0, 0]
    lane = lax.broadcasted_iota(jnp.int32, (1, 128), 1)
    low = lane < 64
    for pair in range(HGROUP // 128):
        cols = slice(pair * 128, (pair + 1) * 128)
        q = q_ref[0, :, cols] * 0.125
        k = k_ref[0, pl.ds(q0, kwin), cols]
        v = v_ref[0, pl.ds(q0, kwin), cols]
        out = None
        for half in range(2):
            sel = low if half == 0 else jnp.logical_not(low)
            qh = jnp.where(sel, q, jnp.zeros_like(q))
            s = lax.dot_general(
                qh, k, (((1,), (1,)), ((), ())), preferred_element_type=jnp.float32
            ) + bias
            m = jnp.max(s, axis=1, keepdims=True)
            p = jnp.exp(s - m)
            total = jnp.sum(p, axis=1, keepdims=True)
            pv = jnp.dot(p.astype(jnp.bfloat16), v, preferred_element_type=jnp.float32)
            pv = pv / total
            out = pv if out is None else jnp.where(low, out, pv)
        o_ref[0, :, cols] = out.astype(o_ref.dtype)


def band_attention(query_enc, keyval, full_bias):
    spec_dev, bin_dev, width = query_enc.shape
    key_span = keyval.shape[1]
    groups = width // HGROUP
    qblocks = bin_dev // QBLOCK
    kwin = QBLOCK + WINDOW
    return pl.pallas_call(
        band_kernel,
        out_shape=jax.ShapeDtypeStruct(query_enc.shape, jnp.bfloat16),
        grid=(spec_dev, groups, qblocks),
        in_specs=[
            pl.BlockSpec((1, QBLOCK, HGROUP), lambda s, g, b: (s, b, g)),
            pl.BlockSpec((1, key_span, HGROUP), lambda s, g, b: (s, 0, g)),
            pl.BlockSpec((1, key_span, HGROUP), lambda s, g, b: (s, 0, groups + g)),
            pl.BlockSpec((1, 1, QBLOCK, kwin), lambda s, g, b: (s, b, 0, 0)),
        ],
        out_specs=pl.BlockSpec((1, QBLOCK, HGROUP), lambda s, g, b: (s, b, g)),
        compiler_params=pltpu.CompilerParams(
            dimension_semantics=("arbitrary", "arbitrary", "arbitrary")
        ),
        cost_estimate=pl.CostEstimate(
            flops=spec_dev * bin_dev * kwin * width * 8,
            transcendentals=spec_dev * bin_dev * kwin * HE,
            bytes_accessed=spec_dev * (bin_dev * width * 4 + key_span * width * 4)
            + full_bias.size * 4,
        ),
    )(query_enc, keyval, keyval, full_bias)


def per_device(
    spectra,
    key_bias,
    valid_bins,
    enc_query,
    enc_key,
    enc_value,
    enc_out,
    token_ids,
    embedding,
    dec_query,
    mem_key,
    mem_value,
    dec_out,
):
    seq_pos = lax.axis_index("seq")
    head_pos = lax.axis_index("head")
    spec_dev, bin_dev, model_width = spectra.shape
    half_span = WINDOW // 2
    first_spec = head_pos * spec_dev
    first_bin = seq_pos * bin_dev
    my_counts = lax.dynamic_slice_in_dim(valid_bins, first_spec, spec_dev, 0)
    bias_pad = jnp.pad(key_bias, ((0, 0), (half_span, half_span)))
    my_bias = lax.dynamic_slice(
        bias_pad, (first_spec, first_bin), (spec_dev, bin_dev + 2 * half_span)
    )
    kv_weights = jnp.concatenate([enc_key, enc_value], axis=1)

    count = lax.axis_size("seq")
    forward = [(i, i + 1) for i in range(count - 1)]
    backward = [(target, source) for source, target in forward]
    low_edge = lax.ppermute(spectra[:, bin_dev - half_span :], "seq", forward)
    high_edge = lax.ppermute(spectra[:, :half_span], "seq", backward)

    normed = rms_rows(spectra)
    query_enc = jnp.einsum(
        "sbd,de->sbe", normed, enc_query, preferred_element_type=jnp.float32
    ).astype(jnp.bfloat16)
    keyval_mid = jnp.einsum(
        "sbd,de->sbe", normed, kv_weights, preferred_element_type=jnp.float32
    ).astype(jnp.bfloat16)
    edges = rms_rows(jnp.concatenate([low_edge, high_edge], axis=1))
    keyval_edges = jnp.einsum(
        "sbd,de->sbe", edges, kv_weights, preferred_element_type=jnp.float32
    ).astype(jnp.bfloat16)
    keyval = jnp.concatenate(
        [keyval_edges[:, :half_span], keyval_mid, keyval_edges[:, half_span:]], axis=1
    )
    key_span = bin_dev + 2 * half_span
    kwin = QBLOCK + WINDOW
    key_cols = first_bin - half_span + jnp.arange(key_span, dtype=jnp.int32)
    col_ok = (key_cols[None, :] >= 0) & (key_cols[None, :] < my_counts[:, None])
    col_bias = jnp.where(col_ok, my_bias, masked_score)
    windows = jnp.stack(
        [col_bias[:, b * QBLOCK : b * QBLOCK + kwin] for b in range(bin_dev // QBLOCK)], axis=1
    )
    offset = (
        jnp.arange(kwin, dtype=jnp.int32)[None, :] - jnp.arange(QBLOCK, dtype=jnp.int32)[:, None]
    )
    band = (offset >= 0) & (offset <= WINDOW)
    full_bias = jnp.where(band[None, None], windows[:, :, None, :], masked_score)
    context = band_attention(query_enc, keyval, full_bias)

    query_rows = first_bin + jnp.arange(bin_dev, dtype=jnp.int32)
    attended = jnp.einsum("sbd,de->sbe", context, enc_out, preferred_element_type=jnp.float32)
    valid_rows = (query_rows[None, :] < my_counts[:, None])[:, :, None]
    encoded = jnp.where(valid_rows, spectra.astype(jnp.float32) + attended, 0.0).astype(
        jnp.bfloat16
    )
    pooled = jnp.mean(
        encoded.astype(jnp.float32).reshape(spec_dev, bin_dev // POOL, POOL, model_width), axis=2
    ).astype(jnp.bfloat16)
    spectra_all = lax.all_gather(pooled, "head", axis=0, tiled=True)
    mem_weights = jnp.concatenate([mem_key, mem_value], axis=1)
    local_width = mem_key.shape[1]
    memory_part = jnp.einsum(
        "spd,de->spe", rms_rows(spectra_all), mem_weights, preferred_element_type=jnp.float32
    ).astype(jnp.bfloat16)
    memory = lax.all_to_all(memory_part, "seq", 0, 1, tiled=True)
    spec_count = key_bias.shape[0]
    mem_len = memory.shape[1]
    bias_row = lax.dynamic_slice_in_dim(key_bias, seq_pos, 1, 0)
    pooled_bias = jnp.max(bias_row.reshape(1, mem_len, POOL), axis=2)
    count_row = lax.dynamic_slice_in_dim(valid_bins, seq_pos, 1, 0)
    mem_valid = jnp.arange(mem_len, dtype=jnp.int32)[None, :] * POOL < count_row[:, None]
    tok_count = token_ids.shape[1]
    dec_width = embedding.shape[1]
    dec_head = dec_width // HD
    heads_here = local_width // dec_head
    onehot = (
        token_ids[:, :, None] == jnp.arange(embedding.shape[0], dtype=jnp.int32)[None, None, :]
    ).astype(jnp.bfloat16)
    hidden = jnp.einsum(
        "stv,vd->std", onehot, embedding, preferred_element_type=jnp.float32
    ).astype(jnp.bfloat16)
    normed_tok = rms_rows(hidden)
    query_dec = jnp.einsum(
        "std,de->ste", normed_tok, dec_query, preferred_element_type=jnp.float32
    ).astype(jnp.bfloat16)
    query_one = lax.all_to_all(query_dec, "seq", 0, 1, tiled=True)
    all_tok = query_one.shape[1]
    query_heads = query_one.reshape(1, all_tok, heads_here, dec_head)
    key_heads = memory[:, :, :local_width].reshape(1, mem_len, heads_here, dec_head)
    value_heads = memory[:, :, local_width:].reshape(1, mem_len, heads_here, dec_head)
    scores = (
        jnp.einsum("sthd,sphd->shtp", query_heads, key_heads, preferred_element_type=jnp.float32)
        * dec_head ** (-0.5)
        + pooled_bias[:, None, None, :]
    )
    scores = jnp.where(mem_valid[:, None, None, :], scores, masked_score)
    weights = softmax_rows(scores)
    context_one = jnp.einsum(
        "shtp,sphd->sthd", weights, value_heads, preferred_element_type=jnp.float32
    ).astype(jnp.bfloat16)
    context_one = context_one.reshape(1, all_tok, local_width)
    dec_context = lax.all_to_all(context_one, "seq", 1, 0, tiled=True)
    share_width = dec_width // lax.axis_size("head")
    partial_sums = jnp.einsum(
        "ste,ed->std", dec_context, dec_out, preferred_element_type=jnp.float32
    )
    summed = lax.psum_scatter(
        partial_sums.astype(jnp.bfloat16), "head", scatter_dimension=2, tiled=True
    ).astype(jnp.float32)
    own_part = lax.dynamic_slice_in_dim(hidden, head_pos * share_width, share_width, 2)
    decoded = (own_part.astype(jnp.float32) + summed).astype(jnp.bfloat16)
    return (encoded, decoded)


def solution(mesh):
    return jax.shard_map(
        per_device,
        mesh=mesh,
        in_specs=(
            P("head", "seq", None),
            P(),
            P(),
            P(),
            P(),
            P(),
            P(),
            P(None, "seq"),
            P(),
            P(None, "head"),
            P(None, "head"),
            P(None, "head"),
            P("head", None),
        ),
        out_specs=(P("head", "seq", None), P(None, "seq", "head")),
        check_vma=False,
    )
```

```python
import jax
import jax.numpy as jnp
from jax import lax
from jax.experimental import pallas as pl
from jax.experimental.pallas import tpu as pltpu
from jax.sharding import PartitionSpec as P

HE = 16
WINDOW = 512
POOL = 32
HD = 32
QBLOCK = 128
HGROUP = 512
DEC_CHUNKS = 2


epsilon = 1e-05
masked_score = -1e30


def rms_rows(values_in):
    widened = values_in.astype(jnp.float32)
    inverse_rms = lax.rsqrt(jnp.mean(widened * widened, axis=-1, keepdims=True) + epsilon)
    return (widened * inverse_rms).astype(jnp.bfloat16)


def softmax_rows(scores):
    row_top = jnp.max(scores, axis=-1, keepdims=True)
    weights = jnp.exp(scores - row_top)
    return (weights / jnp.sum(weights, axis=-1, keepdims=True)).astype(jnp.bfloat16)


def band_kernel(q_ref, k_ref, v_ref, b_ref, o_ref):
    qb = pl.program_id(2)
    q0 = pl.multiple_of(qb * QBLOCK, QBLOCK)
    kwin = QBLOCK + WINDOW
    bias = b_ref[0, 0]
    lane = lax.broadcasted_iota(jnp.int32, (1, 128), 1)
    low = lane < 64
    for pair in range(HGROUP // 128):
        cols = slice(pair * 128, (pair + 1) * 128)
        q = q_ref[0, :, cols] * 0.125
        k = k_ref[0, pl.ds(q0, kwin), cols]
        v = v_ref[0, pl.ds(q0, kwin), cols]
        out = None
        for half in range(2):
            sel = low if half == 0 else jnp.logical_not(low)
            qh = jnp.where(sel, q, jnp.zeros_like(q))
            s = lax.dot_general(
                qh, k, (((1,), (1,)), ((), ())), preferred_element_type=jnp.float32
            ) + bias
            m = jnp.max(s, axis=1, keepdims=True)
            p = jnp.exp(s - m)
            total = jnp.sum(p, axis=1, keepdims=True)
            pv = jnp.dot(p.astype(jnp.bfloat16), v, preferred_element_type=jnp.float32)
            pv = pv / total
            out = pv if out is None else jnp.where(low, out, pv)
        o_ref[0, :, cols] = out.astype(o_ref.dtype)


def band_attention(query_enc, keyval, full_bias):
    spec_dev, bin_dev, width = query_enc.shape
    key_span = keyval.shape[1]
    groups = width // HGROUP
    qblocks = bin_dev // QBLOCK
    kwin = QBLOCK + WINDOW
    return pl.pallas_call(
        band_kernel,
        out_shape=jax.ShapeDtypeStruct(query_enc.shape, jnp.bfloat16),
        grid=(spec_dev, groups, qblocks),
        in_specs=[
            pl.BlockSpec((1, QBLOCK, HGROUP), lambda s, g, b: (s, b, g)),
            pl.BlockSpec((1, key_span, HGROUP), lambda s, g, b: (s, 0, g)),
            pl.BlockSpec((1, key_span, HGROUP), lambda s, g, b: (s, 0, groups + g)),
            pl.BlockSpec((1, 1, QBLOCK, kwin), lambda s, g, b: (s, b, 0, 0)),
        ],
        out_specs=pl.BlockSpec((1, QBLOCK, HGROUP), lambda s, g, b: (s, b, g)),
        compiler_params=pltpu.CompilerParams(
            dimension_semantics=("arbitrary", "arbitrary", "arbitrary")
        ),
        cost_estimate=pl.CostEstimate(
            flops=spec_dev * bin_dev * kwin * width * 8,
            transcendentals=spec_dev * bin_dev * kwin * HE,
            bytes_accessed=spec_dev * (bin_dev * width * 4 + key_span * width * 4)
            + full_bias.size * 4,
        ),
    )(query_enc, keyval, keyval, full_bias)


def per_device(
    spectra,
    key_bias,
    valid_bins,
    enc_query,
    enc_key,
    enc_value,
    enc_out,
    token_ids,
    embedding,
    dec_query,
    mem_key,
    mem_value,
    dec_out,
):
    seq_pos = lax.axis_index("seq")
    head_pos = lax.axis_index("head")
    spec_dev, bin_dev, model_width = spectra.shape
    half_span = WINDOW // 2
    first_spec = head_pos * spec_dev
    first_bin = seq_pos * bin_dev
    my_counts = lax.dynamic_slice_in_dim(valid_bins, first_spec, spec_dev, 0)
    bias_pad = jnp.pad(key_bias, ((0, 0), (half_span, half_span)))
    my_bias = lax.dynamic_slice(
        bias_pad, (first_spec, first_bin), (spec_dev, bin_dev + 2 * half_span)
    )
    kv_weights = jnp.concatenate([enc_key, enc_value], axis=1)

    count = lax.axis_size("seq")
    forward = [(i, i + 1) for i in range(count - 1)]
    backward = [(target, source) for source, target in forward]
    low_edge = lax.ppermute(spectra[:, bin_dev - half_span :], "seq", forward)
    high_edge = lax.ppermute(spectra[:, :half_span], "seq", backward)

    normed = rms_rows(spectra)
    query_enc = jnp.einsum(
        "sbd,de->sbe", normed, enc_query, preferred_element_type=jnp.float32
    ).astype(jnp.bfloat16)
    keyval_mid = jnp.einsum(
        "sbd,de->sbe", normed, kv_weights, preferred_element_type=jnp.float32
    ).astype(jnp.bfloat16)
    edges = rms_rows(jnp.concatenate([low_edge, high_edge], axis=1))
    keyval_edges = jnp.einsum(
        "sbd,de->sbe", edges, kv_weights, preferred_element_type=jnp.float32
    ).astype(jnp.bfloat16)
    keyval = jnp.concatenate(
        [keyval_edges[:, :half_span], keyval_mid, keyval_edges[:, half_span:]], axis=1
    )
    key_span = bin_dev + 2 * half_span
    kwin = QBLOCK + WINDOW
    key_cols = first_bin - half_span + jnp.arange(key_span, dtype=jnp.int32)
    col_ok = (key_cols[None, :] >= 0) & (key_cols[None, :] < my_counts[:, None])
    col_bias = jnp.where(col_ok, my_bias, masked_score)
    windows = jnp.stack(
        [col_bias[:, b * QBLOCK : b * QBLOCK + kwin] for b in range(bin_dev // QBLOCK)], axis=1
    )
    offset = (
        jnp.arange(kwin, dtype=jnp.int32)[None, :] - jnp.arange(QBLOCK, dtype=jnp.int32)[:, None]
    )
    band = (offset >= 0) & (offset <= WINDOW)
    full_bias = jnp.where(band[None, None], windows[:, :, None, :], masked_score)
    context = band_attention(query_enc, keyval, full_bias)

    query_rows = first_bin + jnp.arange(bin_dev, dtype=jnp.int32)
    attended = jnp.einsum("sbd,de->sbe", context, enc_out, preferred_element_type=jnp.float32)
    valid_rows = (query_rows[None, :] < my_counts[:, None])[:, :, None]
    encoded = jnp.where(valid_rows, spectra.astype(jnp.float32) + attended, 0.0).astype(
        jnp.bfloat16
    )
    pooled = jnp.mean(
        encoded.astype(jnp.float32).reshape(spec_dev, bin_dev // POOL, POOL, model_width), axis=2
    ).astype(jnp.bfloat16)
    spectra_all = lax.all_gather(pooled, "head", axis=0, tiled=True)
    mem_weights = jnp.concatenate([mem_key, mem_value], axis=1)
    local_width = mem_key.shape[1]
    memory_part = jnp.einsum(
        "spd,de->spe", rms_rows(spectra_all), mem_weights, preferred_element_type=jnp.float32
    ).astype(jnp.bfloat16)
    memory = lax.all_to_all(memory_part, "seq", 0, 1, tiled=True)
    spec_count = key_bias.shape[0]
    mem_len = memory.shape[1]
    bias_row = lax.dynamic_slice_in_dim(key_bias, seq_pos, 1, 0)
    pooled_bias = jnp.max(bias_row.reshape(1, mem_len, POOL), axis=2)
    count_row = lax.dynamic_slice_in_dim(valid_bins, seq_pos, 1, 0)
    mem_valid = jnp.arange(mem_len, dtype=jnp.int32)[None, :] * POOL < count_row[:, None]
    tok_count = token_ids.shape[1]
    dec_width = embedding.shape[1]
    dec_head = dec_width // HD
    heads_here = local_width // dec_head
    onehot = (
        token_ids[:, :, None] == jnp.arange(embedding.shape[0], dtype=jnp.int32)[None, None, :]
    ).astype(jnp.bfloat16)
    hidden = jnp.einsum(
        "stv,vd->std", onehot, embedding, preferred_element_type=jnp.float32
    ).astype(jnp.bfloat16)
    normed_tok = rms_rows(hidden)
    query_dec = jnp.einsum(
        "std,de->ste", normed_tok, dec_query, preferred_element_type=jnp.float32
    ).astype(jnp.bfloat16)
    query_one = lax.all_to_all(query_dec, "seq", 0, 1, tiled=True)
    seq_count = lax.axis_size("seq")
    query_one = query_one.reshape(seq_count, tok_count, local_width)
    key_heads = memory[:, :, :local_width].reshape(1, mem_len, heads_here, dec_head)
    value_heads = memory[:, :, local_width:].reshape(1, mem_len, heads_here, dec_head)
    share_width = dec_width // lax.axis_size("head")
    own_part = lax.dynamic_slice_in_dim(hidden, head_pos * share_width, share_width, 2)
    sub = tok_count // DEC_CHUNKS
    pieces = []
    for piece in range(DEC_CHUNKS):
        query_piece = query_one[:, piece * sub : (piece + 1) * sub].reshape(
            1, seq_count * sub, heads_here, dec_head
        )
        scores = (
            jnp.einsum(
                "sthd,sphd->shtp", query_piece, key_heads, preferred_element_type=jnp.float32
            )
            * dec_head ** (-0.5)
            + pooled_bias[:, None, None, :]
        )
        scores = jnp.where(mem_valid[:, None, None, :], scores, masked_score)
        weights = softmax_rows(scores)
        context_piece = jnp.einsum(
            "shtp,sphd->sthd", weights, value_heads, preferred_element_type=jnp.float32
        ).astype(jnp.bfloat16)
        context_piece = context_piece.reshape(seq_count, sub, local_width)
        dec_context = lax.all_to_all(context_piece, "seq", 0, 0, tiled=True)
        partial_sums = jnp.einsum(
            "ste,ed->std", dec_context, dec_out, preferred_element_type=jnp.float32
        )
        summed = lax.psum_scatter(
            partial_sums.astype(jnp.bfloat16), "head", scatter_dimension=2, tiled=True
        ).astype(jnp.float32)
        own_piece = own_part[:, piece * sub : (piece + 1) * sub]
        pieces.append((own_piece.astype(jnp.float32) + summed).astype(jnp.bfloat16))
    decoded = jnp.concatenate(pieces, axis=1)
    return (encoded, decoded)


def solution(mesh):
    return jax.shard_map(
        per_device,
        mesh=mesh,
        in_specs=(
            P("head", "seq", None),
            P(),
            P(),
            P(),
            P(),
            P(),
            P(),
            P(None, "seq"),
            P(),
            P(None, "head"),
            P(None, "head"),
            P(None, "head"),
            P("head", None),
        ),
        out_specs=(P("head", "seq", None), P(None, "seq", "head")),
        check_vma=False,
    )
```

```python
import jax
import jax.numpy as jnp
from jax import lax
from jax.experimental import pallas as pl
from jax.experimental.pallas import tpu as pltpu
from jax.sharding import PartitionSpec as P

HE = 16
WINDOW = 512
POOL = 32
HD = 32
QBLOCK = 256
HGROUP = 512


epsilon = 1e-05
masked_score = -1e30


def rms_rows(values_in):
    widened = values_in.astype(jnp.float32)
    inverse_rms = lax.rsqrt(jnp.mean(widened * widened, axis=-1, keepdims=True) + epsilon)
    return (widened * inverse_rms).astype(jnp.bfloat16)


def softmax_rows(scores):
    row_top = jnp.max(scores, axis=-1, keepdims=True)
    weights = jnp.exp(scores - row_top)
    return (weights / jnp.sum(weights, axis=-1, keepdims=True)).astype(jnp.bfloat16)


def band_kernel(q_ref, k_ref, v_ref, b_ref, o_ref):
    qb = pl.program_id(2)
    q0 = pl.multiple_of(qb * QBLOCK, QBLOCK)
    kwin = QBLOCK + WINDOW
    bias = b_ref[0, 0]
    lane = lax.broadcasted_iota(jnp.int32, (1, 128), 1)
    low = lane < 64
    for pair in range(HGROUP // 128):
        cols = slice(pair * 128, (pair + 1) * 128)
        q = q_ref[0, :, cols] * 0.125
        k = k_ref[0, pl.ds(q0, kwin), cols]
        v = v_ref[0, pl.ds(q0, kwin), cols]
        out = None
        for half in range(2):
            sel = low if half == 0 else jnp.logical_not(low)
            qh = jnp.where(sel, q, jnp.zeros_like(q))
            s = lax.dot_general(
                qh, k, (((1,), (1,)), ((), ())), preferred_element_type=jnp.float32
            ) + bias
            m = jnp.max(s, axis=1, keepdims=True)
            p = jnp.exp(s - m)
            total = jnp.sum(p, axis=1, keepdims=True)
            pv = jnp.dot(p.astype(jnp.bfloat16), v, preferred_element_type=jnp.float32)
            pv = pv / total
            out = pv if out is None else jnp.where(low, out, pv)
        o_ref[0, :, cols] = out.astype(o_ref.dtype)


def band_attention(query_enc, keyval, full_bias):
    spec_dev, bin_dev, width = query_enc.shape
    key_span = keyval.shape[1]
    groups = width // HGROUP
    qblocks = bin_dev // QBLOCK
    kwin = QBLOCK + WINDOW
    return pl.pallas_call(
        band_kernel,
        out_shape=jax.ShapeDtypeStruct(query_enc.shape, jnp.bfloat16),
        grid=(spec_dev, groups, qblocks),
        in_specs=[
            pl.BlockSpec((1, QBLOCK, HGROUP), lambda s, g, b: (s, b, g)),
            pl.BlockSpec((1, key_span, HGROUP), lambda s, g, b: (s, 0, g)),
            pl.BlockSpec((1, key_span, HGROUP), lambda s, g, b: (s, 0, groups + g)),
            pl.BlockSpec((1, 1, QBLOCK, kwin), lambda s, g, b: (s, b, 0, 0)),
        ],
        out_specs=pl.BlockSpec((1, QBLOCK, HGROUP), lambda s, g, b: (s, b, g)),
        compiler_params=pltpu.CompilerParams(
            dimension_semantics=("arbitrary", "arbitrary", "arbitrary")
        ),
        cost_estimate=pl.CostEstimate(
            flops=spec_dev * bin_dev * kwin * width * 8,
            transcendentals=spec_dev * bin_dev * kwin * HE,
            bytes_accessed=spec_dev * (bin_dev * width * 4 + key_span * width * 4)
            + full_bias.size * 4,
        ),
    )(query_enc, keyval, keyval, full_bias)


def per_device(
    spectra,
    key_bias,
    valid_bins,
    enc_query,
    enc_key,
    enc_value,
    enc_out,
    token_ids,
    embedding,
    dec_query,
    mem_key,
    mem_value,
    dec_out,
):
    seq_pos = lax.axis_index("seq")
    head_pos = lax.axis_index("head")
    spec_dev, bin_dev, model_width = spectra.shape
    half_span = WINDOW // 2
    first_spec = head_pos * spec_dev
    first_bin = seq_pos * bin_dev
    my_counts = lax.dynamic_slice_in_dim(valid_bins, first_spec, spec_dev, 0)
    bias_pad = jnp.pad(key_bias, ((0, 0), (half_span, half_span)))
    my_bias = lax.dynamic_slice(
        bias_pad, (first_spec, first_bin), (spec_dev, bin_dev + 2 * half_span)
    )
    kv_weights = jnp.concatenate([enc_key, enc_value], axis=1)

    count = lax.axis_size("seq")
    forward = [(i, i + 1) for i in range(count - 1)]
    backward = [(target, source) for source, target in forward]
    low_edge = lax.ppermute(spectra[:, bin_dev - half_span :], "seq", forward)
    high_edge = lax.ppermute(spectra[:, :half_span], "seq", backward)

    normed = rms_rows(spectra)
    query_enc = jnp.einsum(
        "sbd,de->sbe", normed, enc_query, preferred_element_type=jnp.float32
    ).astype(jnp.bfloat16)
    keyval_mid = jnp.einsum(
        "sbd,de->sbe", normed, kv_weights, preferred_element_type=jnp.float32
    ).astype(jnp.bfloat16)
    edges = rms_rows(jnp.concatenate([low_edge, high_edge], axis=1))
    keyval_edges = jnp.einsum(
        "sbd,de->sbe", edges, kv_weights, preferred_element_type=jnp.float32
    ).astype(jnp.bfloat16)
    keyval = jnp.concatenate(
        [keyval_edges[:, :half_span], keyval_mid, keyval_edges[:, half_span:]], axis=1
    )
    key_span = bin_dev + 2 * half_span
    kwin = QBLOCK + WINDOW
    key_cols = first_bin - half_span + jnp.arange(key_span, dtype=jnp.int32)
    col_ok = (key_cols[None, :] >= 0) & (key_cols[None, :] < my_counts[:, None])
    col_bias = jnp.where(col_ok, my_bias, masked_score)
    windows = jnp.stack(
        [col_bias[:, b * QBLOCK : b * QBLOCK + kwin] for b in range(bin_dev // QBLOCK)], axis=1
    )
    offset = (
        jnp.arange(kwin, dtype=jnp.int32)[None, :] - jnp.arange(QBLOCK, dtype=jnp.int32)[:, None]
    )
    band = (offset >= 0) & (offset <= WINDOW)
    full_bias = jnp.where(band[None, None], windows[:, :, None, :], masked_score)
    context = band_attention(query_enc, keyval, full_bias)

    query_rows = first_bin + jnp.arange(bin_dev, dtype=jnp.int32)
    attended = jnp.einsum("sbd,de->sbe", context, enc_out, preferred_element_type=jnp.float32)
    valid_rows = (query_rows[None, :] < my_counts[:, None])[:, :, None]
    encoded = jnp.where(valid_rows, spectra.astype(jnp.float32) + attended, 0.0).astype(
        jnp.bfloat16
    )
    pooled = jnp.mean(
        encoded.astype(jnp.float32).reshape(spec_dev, bin_dev // POOL, POOL, model_width), axis=2
    ).astype(jnp.bfloat16)
    spectra_all = lax.all_gather(pooled, "head", axis=0, tiled=True)
    mem_weights = jnp.concatenate([mem_key, mem_value], axis=1)
    local_width = mem_key.shape[1]
    memory_part = jnp.einsum(
        "spd,de->spe", rms_rows(spectra_all), mem_weights, preferred_element_type=jnp.float32
    ).astype(jnp.bfloat16)
    memory = lax.all_to_all(memory_part, "seq", 0, 1, tiled=True)
    spec_count = key_bias.shape[0]
    mem_len = memory.shape[1]
    bias_row = lax.dynamic_slice_in_dim(key_bias, seq_pos, 1, 0)
    pooled_bias = jnp.max(bias_row.reshape(1, mem_len, POOL), axis=2)
    count_row = lax.dynamic_slice_in_dim(valid_bins, seq_pos, 1, 0)
    mem_valid = jnp.arange(mem_len, dtype=jnp.int32)[None, :] * POOL < count_row[:, None]
    tok_count = token_ids.shape[1]
    dec_width = embedding.shape[1]
    dec_head = dec_width // HD
    heads_here = local_width // dec_head
    share_width = dec_width // lax.axis_size("head")
    vocab = embedding.shape[0]
    onehot = (
        token_ids[:, :, None] == jnp.arange(vocab, dtype=jnp.int32)[None, None, :]
    ).astype(jnp.bfloat16)
    own_table = lax.dynamic_slice_in_dim(embedding, head_pos * share_width, share_width, 1)
    own_part = jnp.einsum(
        "stv,vd->std", onehot, own_table, preferred_element_type=jnp.float32
    ).astype(jnp.bfloat16)
    ids_all = lax.all_gather(token_ids, "seq", axis=1, tiled=True)
    ids_one = lax.dynamic_slice_in_dim(ids_all, seq_pos, 1, 0)
    onehot_one = (
        ids_one[:, :, None] == jnp.arange(vocab, dtype=jnp.int32)[None, None, :]
    ).astype(jnp.bfloat16)
    hidden_one = jnp.einsum(
        "stv,vd->std", onehot_one, embedding, preferred_element_type=jnp.float32
    ).astype(jnp.bfloat16)
    query_one = jnp.einsum(
        "std,de->ste", rms_rows(hidden_one), dec_query, preferred_element_type=jnp.float32
    ).astype(jnp.bfloat16)
    all_tok = query_one.shape[1]
    query_heads = query_one.reshape(1, all_tok, heads_here, dec_head)
    key_heads = memory[:, :, :local_width].reshape(1, mem_len, heads_here, dec_head)
    value_heads = memory[:, :, local_width:].reshape(1, mem_len, heads_here, dec_head)
    scores = (
        jnp.einsum("sthd,sphd->shtp", query_heads, key_heads, preferred_element_type=jnp.float32)
        * dec_head ** (-0.5)
        + pooled_bias[:, None, None, :]
    )
    scores = jnp.where(mem_valid[:, None, None, :], scores, masked_score)
    weights = softmax_rows(scores)
    context_one = jnp.einsum(
        "shtp,sphd->sthd", weights, value_heads, preferred_element_type=jnp.float32
    ).astype(jnp.bfloat16)
    context_one = context_one.reshape(1, all_tok, local_width)
    dec_context = lax.all_to_all(context_one, "seq", 1, 0, tiled=True)
    partial_sums = jnp.einsum(
        "ste,ed->std", dec_context, dec_out, preferred_element_type=jnp.float32
    )
    summed = lax.psum_scatter(
        partial_sums.astype(jnp.bfloat16), "head", scatter_dimension=2, tiled=True
    ).astype(jnp.float32)
    decoded = (own_part.astype(jnp.float32) + summed).astype(jnp.bfloat16)
    return (encoded, decoded)


def solution(mesh):
    return jax.shard_map(
        per_device,
        mesh=mesh,
        in_specs=(
            P("head", "seq", None),
            P(),
            P(),
            P(),
            P(),
            P(),
            P(),
            P(None, "seq"),
            P(),
            P(None, "head"),
            P(None, "head"),
            P(None, "head"),
            P("head", None),
        ),
        out_specs=(P("head", "seq", None), P(None, "seq", "head")),
        check_vma=False,
    )
```

```python
import jax
import jax.numpy as jnp
from jax import lax
from jax.experimental import pallas as pl
from jax.experimental.pallas import tpu as pltpu
from jax.sharding import PartitionSpec as P

HE = 16
WINDOW = 512
POOL = 32
HD = 32
QBLOCK = 256
HGROUP = 512


epsilon = 1e-05
masked_score = -1e30


def rms_rows(values_in):
    widened = values_in.astype(jnp.float32)
    inverse_rms = lax.rsqrt(jnp.mean(widened * widened, axis=-1, keepdims=True) + epsilon)
    return (widened * inverse_rms).astype(jnp.bfloat16)


def softmax_rows(scores):
    row_top = jnp.max(scores, axis=-1, keepdims=True)
    weights = jnp.exp(scores - row_top)
    return (weights / jnp.sum(weights, axis=-1, keepdims=True)).astype(jnp.bfloat16)


def band_kernel(q_ref, k_ref, v_ref, b_ref, o_ref):
    qb = pl.program_id(2)
    q0 = pl.multiple_of(qb * QBLOCK, QBLOCK)
    kwin = QBLOCK + WINDOW
    bias = b_ref[0, 0]
    lane = lax.broadcasted_iota(jnp.int32, (1, 128), 1)
    low = lane < 64
    for pair in range(HGROUP // 128):
        cols = slice(pair * 128, (pair + 1) * 128)
        q = q_ref[0, :, cols] * 0.125
        k = k_ref[0, pl.ds(q0, kwin), cols]
        v = v_ref[0, pl.ds(q0, kwin), cols]
        out = None
        for half in range(2):
            sel = low if half == 0 else jnp.logical_not(low)
            qh = jnp.where(sel, q, jnp.zeros_like(q))
            s = lax.dot_general(
                qh, k, (((1,), (1,)), ((), ())), preferred_element_type=jnp.float32
            ) + bias
            m = jnp.max(s, axis=1, keepdims=True)
            p = jnp.exp(s - m)
            total = jnp.sum(p, axis=1, keepdims=True)
            pv = jnp.dot(p.astype(jnp.bfloat16), v, preferred_element_type=jnp.float32)
            pv = pv / total
            out = pv if out is None else jnp.where(low, out, pv)
        o_ref[0, :, cols] = out.astype(o_ref.dtype)


def band_attention(query_enc, keyval, full_bias):
    spec_dev, bin_dev, width = query_enc.shape
    key_span = keyval.shape[1]
    groups = width // HGROUP
    qblocks = bin_dev // QBLOCK
    kwin = QBLOCK + WINDOW
    return pl.pallas_call(
        band_kernel,
        out_shape=jax.ShapeDtypeStruct(query_enc.shape, jnp.bfloat16),
        grid=(spec_dev, groups, qblocks),
        in_specs=[
            pl.BlockSpec((1, QBLOCK, HGROUP), lambda s, g, b: (s, b, g)),
            pl.BlockSpec((1, key_span, HGROUP), lambda s, g, b: (s, 0, g)),
            pl.BlockSpec((1, key_span, HGROUP), lambda s, g, b: (s, 0, groups + g)),
            pl.BlockSpec((1, 1, QBLOCK, kwin), lambda s, g, b: (s, b, 0, 0)),
        ],
        out_specs=pl.BlockSpec((1, QBLOCK, HGROUP), lambda s, g, b: (s, b, g)),
        compiler_params=pltpu.CompilerParams(
            dimension_semantics=("arbitrary", "arbitrary", "arbitrary")
        ),
        cost_estimate=pl.CostEstimate(
            flops=spec_dev * bin_dev * kwin * width * 8,
            transcendentals=spec_dev * bin_dev * kwin * HE,
            bytes_accessed=spec_dev * (bin_dev * width * 4 + key_span * width * 4)
            + full_bias.size * 4,
        ),
    )(query_enc, keyval, keyval, full_bias)


def per_device(
    spectra,
    key_bias,
    valid_bins,
    enc_query,
    enc_key,
    enc_value,
    enc_out,
    token_ids,
    embedding,
    dec_query,
    mem_key,
    mem_value,
    dec_out,
):
    seq_pos = lax.axis_index("seq")
    head_pos = lax.axis_index("head")
    spec_dev, bin_dev, model_width = spectra.shape
    half_span = WINDOW // 2
    first_spec = head_pos * spec_dev
    first_bin = seq_pos * bin_dev
    my_counts = lax.dynamic_slice_in_dim(valid_bins, first_spec, spec_dev, 0)
    bias_pad = jnp.pad(key_bias, ((0, 0), (half_span, half_span)))
    my_bias = lax.dynamic_slice(
        bias_pad, (first_spec, first_bin), (spec_dev, bin_dev + 2 * half_span)
    )
    kv_weights = jnp.concatenate([enc_key, enc_value], axis=1)

    count = lax.axis_size("seq")
    forward = [(i, i + 1) for i in range(count - 1)]
    backward = [(target, source) for source, target in forward]
    low_edge = lax.ppermute(spectra[:, bin_dev - half_span :], "seq", forward)
    high_edge = lax.ppermute(spectra[:, :half_span], "seq", backward)

    normed = rms_rows(spectra)
    query_enc = jnp.einsum(
        "sbd,de->sbe", normed, enc_query, preferred_element_type=jnp.float32
    ).astype(jnp.bfloat16)
    keyval_mid = jnp.einsum(
        "sbd,de->sbe", normed, kv_weights, preferred_element_type=jnp.float32
    ).astype(jnp.bfloat16)
    edges = rms_rows(jnp.concatenate([low_edge, high_edge], axis=1))
    keyval_edges = jnp.einsum(
        "sbd,de->sbe", edges, kv_weights, preferred_element_type=jnp.float32
    ).astype(jnp.bfloat16)
    keyval = jnp.concatenate(
        [keyval_edges[:, :half_span], keyval_mid, keyval_edges[:, half_span:]], axis=1
    )
    key_span = bin_dev + 2 * half_span
    kwin = QBLOCK + WINDOW
    key_cols = first_bin - half_span + jnp.arange(key_span, dtype=jnp.int32)
    col_ok = (key_cols[None, :] >= 0) & (key_cols[None, :] < my_counts[:, None])
    col_bias = jnp.where(col_ok, my_bias, masked_score)
    windows = jnp.stack(
        [col_bias[:, b * QBLOCK : b * QBLOCK + kwin] for b in range(bin_dev // QBLOCK)], axis=1
    )
    offset = (
        jnp.arange(kwin, dtype=jnp.int32)[None, :] - jnp.arange(QBLOCK, dtype=jnp.int32)[:, None]
    )
    band = (offset >= 0) & (offset <= WINDOW)
    full_bias = jnp.where(band[None, None], windows[:, :, None, :], masked_score)
    context = band_attention(query_enc, keyval, full_bias)

    query_rows = first_bin + jnp.arange(bin_dev, dtype=jnp.int32)
    attended = jnp.einsum("sbd,de->sbe", context, enc_out, preferred_element_type=jnp.float32)
    valid_rows = (query_rows[None, :] < my_counts[:, None])[:, :, None]
    encoded = jnp.where(valid_rows, spectra.astype(jnp.float32) + attended, 0.0).astype(
        jnp.bfloat16
    )
    pooled = jnp.mean(
        encoded.astype(jnp.float32).reshape(spec_dev, bin_dev // POOL, POOL, model_width), axis=2
    ).astype(jnp.bfloat16)
    spectra_all = lax.all_gather(pooled, "head", axis=0, tiled=True)
    mem_weights = jnp.concatenate([mem_key, mem_value], axis=1)
    local_width = mem_key.shape[1]
    memory_part = jnp.einsum(
        "spd,de->spe", rms_rows(spectra_all), mem_weights, preferred_element_type=jnp.float32
    ).astype(jnp.bfloat16)
    spec_count, part_len, part_width = memory_part.shape
    tok_count = token_ids.shape[1]
    id_rows = jnp.zeros((spec_count, 1, part_width), jnp.bfloat16)
    id_rows = id_rows.at[:, 0, :tok_count].set(token_ids.astype(jnp.bfloat16))
    payload = jnp.concatenate([memory_part, id_rows], axis=1)
    received = lax.all_to_all(payload, "seq", 0, 1, tiled=True)
    seq_count = lax.axis_size("seq")
    received = received.reshape(seq_count, part_len + 1, part_width)
    memory = received[:, :part_len].reshape(1, seq_count * part_len, part_width)
    ids_one = received[:, part_len, :tok_count].reshape(1, seq_count * tok_count)
    ids_one = ids_one.astype(jnp.int32)
    mem_len = memory.shape[1]
    bias_row = lax.dynamic_slice_in_dim(key_bias, seq_pos, 1, 0)
    pooled_bias = jnp.max(bias_row.reshape(1, mem_len, POOL), axis=2)
    count_row = lax.dynamic_slice_in_dim(valid_bins, seq_pos, 1, 0)
    mem_valid = jnp.arange(mem_len, dtype=jnp.int32)[None, :] * POOL < count_row[:, None]
    dec_width = embedding.shape[1]
    dec_head = dec_width // HD
    heads_here = local_width // dec_head
    share_width = dec_width // lax.axis_size("head")
    vocab = embedding.shape[0]
    onehot = (
        token_ids[:, :, None] == jnp.arange(vocab, dtype=jnp.int32)[None, None, :]
    ).astype(jnp.bfloat16)
    own_table = lax.dynamic_slice_in_dim(embedding, head_pos * share_width, share_width, 1)
    own_part = jnp.einsum(
        "stv,vd->std", onehot, own_table, preferred_element_type=jnp.float32
    ).astype(jnp.bfloat16)
    onehot_one = (
        ids_one[:, :, None] == jnp.arange(vocab, dtype=jnp.int32)[None, None, :]
    ).astype(jnp.bfloat16)
    hidden_one = jnp.einsum(
        "stv,vd->std", onehot_one, embedding, preferred_element_type=jnp.float32
    ).astype(jnp.bfloat16)
    query_one = jnp.einsum(
        "std,de->ste", rms_rows(hidden_one), dec_query, preferred_element_type=jnp.float32
    ).astype(jnp.bfloat16)
    all_tok = query_one.shape[1]
    query_heads = query_one.reshape(1, all_tok, heads_here, dec_head)
    key_heads = memory[:, :, :local_width].reshape(1, mem_len, heads_here, dec_head)
    value_heads = memory[:, :, local_width:].reshape(1, mem_len, heads_here, dec_head)
    scores = (
        jnp.einsum("sthd,sphd->shtp", query_heads, key_heads, preferred_element_type=jnp.float32)
        * dec_head ** (-0.5)
        + pooled_bias[:, None, None, :]
    )
    scores = jnp.where(mem_valid[:, None, None, :], scores, masked_score)
    weights = softmax_rows(scores)
    context_one = jnp.einsum(
        "shtp,sphd->sthd", weights, value_heads, preferred_element_type=jnp.float32
    ).astype(jnp.bfloat16)
    context_one = context_one.reshape(1, all_tok, local_width)
    dec_context = lax.all_to_all(context_one, "seq", 1, 0, tiled=True)
    partial_sums = jnp.einsum(
        "ste,ed->std", dec_context, dec_out, preferred_element_type=jnp.float32
    )
    summed = lax.psum_scatter(
        partial_sums.astype(jnp.bfloat16), "head", scatter_dimension=2, tiled=True
    ).astype(jnp.float32)
    decoded = (own_part.astype(jnp.float32) + summed).astype(jnp.bfloat16)
    return (encoded, decoded)


def solution(mesh):
    return jax.shard_map(
        per_device,
        mesh=mesh,
        in_specs=(
            P("head", "seq", None),
            P(),
            P(),
            P(),
            P(),
            P(),
            P(),
            P(None, "seq"),
            P(),
            P(None, "head"),
            P(None, "head"),
            P(None, "head"),
            P("head", None),
        ),
        out_specs=(P("head", "seq", None), P(None, "seq", "head")),
        check_vma=False,
    )
```

```python
import jax
import jax.numpy as jnp
from jax import lax
from jax.experimental import pallas as pl
from jax.experimental.pallas import tpu as pltpu
from jax.sharding import PartitionSpec as P

HE = 16
WINDOW = 512
POOL = 32
HD = 32
QBLOCK = 256
HGROUP = 512


epsilon = 1e-05
masked_score = -1e30


def rms_rows(values_in):
    widened = values_in.astype(jnp.float32)
    inverse_rms = lax.rsqrt(jnp.mean(widened * widened, axis=-1, keepdims=True) + epsilon)
    return (widened * inverse_rms).astype(jnp.bfloat16)


def softmax_rows(scores):
    row_top = jnp.max(scores, axis=-1, keepdims=True)
    weights = jnp.exp(scores - row_top)
    return (weights / jnp.sum(weights, axis=-1, keepdims=True)).astype(jnp.bfloat16)


def band_kernel(q_ref, k_ref, v_ref, b_ref, o_ref):
    qb = pl.program_id(2)
    q0 = pl.multiple_of(qb * QBLOCK, QBLOCK)
    kwin = QBLOCK + WINDOW
    bias = b_ref[0, 0]
    lane = lax.broadcasted_iota(jnp.int32, (1, 128), 1)
    low = lane < 64
    for pair in range(HGROUP // 128):
        cols = slice(pair * 128, (pair + 1) * 128)
        q = q_ref[0, :, cols] * 0.125
        k = k_ref[0, pl.ds(q0, kwin), cols]
        v = v_ref[0, pl.ds(q0, kwin), cols]
        out = None
        for half in range(2):
            sel = low if half == 0 else jnp.logical_not(low)
            qh = jnp.where(sel, q, jnp.zeros_like(q))
            s = lax.dot_general(
                qh, k, (((1,), (1,)), ((), ())), preferred_element_type=jnp.float32
            ) + bias
            m = jnp.max(s, axis=1, keepdims=True)
            p = jnp.exp(s - m)
            total = jnp.sum(p, axis=1, keepdims=True)
            pv = jnp.dot(p.astype(jnp.bfloat16), v, preferred_element_type=jnp.float32)
            pv = pv / total
            out = pv if out is None else jnp.where(low, out, pv)
        o_ref[0, :, cols] = out.astype(o_ref.dtype)


def band_attention(query_enc, keyval, full_bias):
    spec_dev, bin_dev, width = query_enc.shape
    key_span = keyval.shape[1]
    groups = width // HGROUP
    qblocks = bin_dev // QBLOCK
    kwin = QBLOCK + WINDOW
    return pl.pallas_call(
        band_kernel,
        out_shape=jax.ShapeDtypeStruct(query_enc.shape, jnp.bfloat16),
        grid=(spec_dev, groups, qblocks),
        in_specs=[
            pl.BlockSpec((1, QBLOCK, HGROUP), lambda s, g, b: (s, b, g)),
            pl.BlockSpec((1, key_span, HGROUP), lambda s, g, b: (s, 0, g)),
            pl.BlockSpec((1, key_span, HGROUP), lambda s, g, b: (s, 0, groups + g)),
            pl.BlockSpec((1, 1, QBLOCK, kwin), lambda s, g, b: (s, b, 0, 0)),
        ],
        out_specs=pl.BlockSpec((1, QBLOCK, HGROUP), lambda s, g, b: (s, b, g)),
        compiler_params=pltpu.CompilerParams(
            dimension_semantics=("arbitrary", "arbitrary", "arbitrary")
        ),
        cost_estimate=pl.CostEstimate(
            flops=spec_dev * bin_dev * kwin * width * 8,
            transcendentals=spec_dev * bin_dev * kwin * HE,
            bytes_accessed=spec_dev * (bin_dev * width * 4 + key_span * width * 4)
            + full_bias.size * 4,
        ),
    )(query_enc, keyval, keyval, full_bias)


def per_device(
    spectra,
    key_bias,
    valid_bins,
    enc_query,
    enc_key,
    enc_value,
    enc_out,
    token_ids,
    embedding,
    dec_query,
    mem_key,
    mem_value,
    dec_out,
):
    seq_pos = lax.axis_index("seq")
    head_pos = lax.axis_index("head")
    spec_dev, bin_dev, model_width = spectra.shape
    half_span = WINDOW // 2
    first_spec = head_pos * spec_dev
    first_bin = seq_pos * bin_dev
    my_counts = lax.dynamic_slice_in_dim(valid_bins, first_spec, spec_dev, 0)
    bias_pad = jnp.pad(key_bias, ((0, 0), (half_span, half_span)))
    my_bias = lax.dynamic_slice(
        bias_pad, (first_spec, first_bin), (spec_dev, bin_dev + 2 * half_span)
    )
    kv_weights = jnp.concatenate([enc_key, enc_value], axis=1)

    count = lax.axis_size("seq")
    forward = [(i, i + 1) for i in range(count - 1)]
    backward = [(target, source) for source, target in forward]
    low_edge = lax.ppermute(spectra[:, bin_dev - half_span :], "seq", forward)
    high_edge = lax.ppermute(spectra[:, :half_span], "seq", backward)

    normed = rms_rows(spectra)
    query_enc = jnp.einsum(
        "sbd,de->sbe", normed, enc_query, preferred_element_type=jnp.float32
    ).astype(jnp.bfloat16)
    keyval_mid = jnp.einsum(
        "sbd,de->sbe", normed, kv_weights, preferred_element_type=jnp.float32
    ).astype(jnp.bfloat16)
    edges = rms_rows(jnp.concatenate([low_edge, high_edge], axis=1))
    keyval_edges = jnp.einsum(
        "sbd,de->sbe", edges, kv_weights, preferred_element_type=jnp.float32
    ).astype(jnp.bfloat16)
    keyval = jnp.concatenate(
        [keyval_edges[:, :half_span], keyval_mid, keyval_edges[:, half_span:]], axis=1
    )
    key_span = bin_dev + 2 * half_span
    kwin = QBLOCK + WINDOW
    key_cols = first_bin - half_span + jnp.arange(key_span, dtype=jnp.int32)
    col_ok = (key_cols[None, :] >= 0) & (key_cols[None, :] < my_counts[:, None])
    col_bias = jnp.where(col_ok, my_bias, masked_score)
    windows = jnp.stack(
        [col_bias[:, b * QBLOCK : b * QBLOCK + kwin] for b in range(bin_dev // QBLOCK)], axis=1
    )
    offset = (
        jnp.arange(kwin, dtype=jnp.int32)[None, :] - jnp.arange(QBLOCK, dtype=jnp.int32)[:, None]
    )
    band = (offset >= 0) & (offset <= WINDOW)
    full_bias = jnp.where(band[None, None], windows[:, :, None, :], masked_score)
    context = band_attention(query_enc, keyval, full_bias)

    query_rows = first_bin + jnp.arange(bin_dev, dtype=jnp.int32)
    attended = jnp.einsum("sbd,de->sbe", context, enc_out, preferred_element_type=jnp.float32)
    valid_rows = (query_rows[None, :] < my_counts[:, None])[:, :, None]
    encoded = jnp.where(valid_rows, spectra.astype(jnp.float32) + attended, 0.0).astype(
        jnp.bfloat16
    )
    pooled = jnp.mean(
        encoded.astype(jnp.float32).reshape(spec_dev, bin_dev // POOL, POOL, model_width), axis=2
    ).astype(jnp.bfloat16)
    spectra_all = lax.all_gather(pooled, "head", axis=0, tiled=True)
    mem_weights = jnp.concatenate([mem_key, mem_value], axis=1)
    local_width = mem_key.shape[1]
    memory_part = jnp.einsum(
        "spd,de->spe", rms_rows(spectra_all), mem_weights, preferred_element_type=jnp.float32
    ).astype(jnp.bfloat16)
    spec_count, part_len, part_width = memory_part.shape
    tok_count = token_ids.shape[1]
    id_cols = jnp.zeros((spec_count, part_len, 128), jnp.bfloat16)
    id_cols = id_cols.at[:, 0, :tok_count].set(token_ids.astype(jnp.bfloat16))
    payload = jnp.concatenate([memory_part, id_cols], axis=2)
    received = lax.all_to_all(payload, "seq", 0, 1, tiled=True)
    seq_count = lax.axis_size("seq")
    memory = received[:, :, :part_width]
    ids_one = received.reshape(seq_count, part_len, part_width + 128)[:, 0, part_width : part_width + tok_count]
    ids_one = ids_one.reshape(1, seq_count * tok_count).astype(jnp.int32)
    mem_len = memory.shape[1]
    bias_row = lax.dynamic_slice_in_dim(key_bias, seq_pos, 1, 0)
    pooled_bias = jnp.max(bias_row.reshape(1, mem_len, POOL), axis=2)
    count_row = lax.dynamic_slice_in_dim(valid_bins, seq_pos, 1, 0)
    mem_valid = jnp.arange(mem_len, dtype=jnp.int32)[None, :] * POOL < count_row[:, None]
    dec_width = embedding.shape[1]
    dec_head = dec_width // HD
    heads_here = local_width // dec_head
    share_width = dec_width // lax.axis_size("head")
    vocab = embedding.shape[0]
    onehot = (
        token_ids[:, :, None] == jnp.arange(vocab, dtype=jnp.int32)[None, None, :]
    ).astype(jnp.bfloat16)
    own_table = lax.dynamic_slice_in_dim(embedding, head_pos * share_width, share_width, 1)
    own_part = jnp.einsum(
        "stv,vd->std", onehot, own_table, preferred_element_type=jnp.float32
    ).astype(jnp.bfloat16)
    onehot_one = (
        ids_one[:, :, None] == jnp.arange(vocab, dtype=jnp.int32)[None, None, :]
    ).astype(jnp.bfloat16)
    query_table = jnp.einsum(
        "vd,de->ve", rms_rows(embedding), dec_query, preferred_element_type=jnp.float32
    ).astype(jnp.bfloat16)
    query_one = jnp.einsum(
        "stv,ve->ste", onehot_one, query_table, preferred_element_type=jnp.float32
    ).astype(jnp.bfloat16)
    all_tok = query_one.shape[1]
    query_heads = query_one.reshape(1, all_tok, heads_here, dec_head)
    key_heads = memory[:, :, :local_width].reshape(1, mem_len, heads_here, dec_head)
    value_heads = memory[:, :, local_width:].reshape(1, mem_len, heads_here, dec_head)
    scores = (
        jnp.einsum("sthd,sphd->shtp", query_heads, key_heads, preferred_element_type=jnp.float32)
        * dec_head ** (-0.5)
        + pooled_bias[:, None, None, :]
    )
    scores = jnp.where(mem_valid[:, None, None, :], scores, masked_score)
    weights = softmax_rows(scores)
    context_one = jnp.einsum(
        "shtp,sphd->sthd", weights, value_heads, preferred_element_type=jnp.float32
    ).astype(jnp.bfloat16)
    context_one = context_one.reshape(1, all_tok, local_width)
    dec_context = lax.all_to_all(context_one, "seq", 1, 0, tiled=True)
    partial_sums = jnp.einsum(
        "ste,ed->std", dec_context, dec_out, preferred_element_type=jnp.float32
    )
    summed = lax.psum_scatter(
        partial_sums.astype(jnp.bfloat16), "head", scatter_dimension=2, tiled=True
    ).astype(jnp.float32)
    decoded = (own_part.astype(jnp.float32) + summed).astype(jnp.bfloat16)
    return (encoded, decoded)


def solution(mesh):
    return jax.shard_map(
        per_device,
        mesh=mesh,
        in_specs=(
            P("head", "seq", None),
            P(),
            P(),
            P(),
            P(),
            P(),
            P(),
            P(None, "seq"),
            P(),
            P(None, "head"),
            P(None, "head"),
            P(None, "head"),
            P("head", None),
        ),
        out_specs=(P("head", "seq", None), P(None, "seq", "head")),
        check_vma=False,
    )
```

```python
import jax
import jax.numpy as jnp
from jax import lax
from jax.experimental import pallas as pl
from jax.experimental.pallas import tpu as pltpu
from jax.sharding import PartitionSpec as P

HE = 16
WINDOW = 512
POOL = 32
HD = 32
QBLOCK = 256
HGROUP = 512
DEC_SCALE = 128 ** (-0.5)


epsilon = 1e-05
masked_score = -1e30


def rms_rows(values_in):
    widened = values_in.astype(jnp.float32)
    inverse_rms = lax.rsqrt(jnp.mean(widened * widened, axis=-1, keepdims=True) + epsilon)
    return (widened * inverse_rms).astype(jnp.bfloat16)


def softmax_rows(scores):
    row_top = jnp.max(scores, axis=-1, keepdims=True)
    weights = jnp.exp(scores - row_top)
    return (weights / jnp.sum(weights, axis=-1, keepdims=True)).astype(jnp.bfloat16)


def band_kernel(q_ref, k_ref, v_ref, b_ref, o_ref):
    qb = pl.program_id(2)
    q0 = pl.multiple_of(qb * QBLOCK, QBLOCK)
    kwin = QBLOCK + WINDOW
    bias = b_ref[0, 0]
    lane = lax.broadcasted_iota(jnp.int32, (1, 128), 1)
    low = lane < 64
    for pair in range(HGROUP // 128):
        cols = slice(pair * 128, (pair + 1) * 128)
        q = q_ref[0, :, cols] * 0.125
        k = k_ref[0, pl.ds(q0, kwin), cols]
        v = v_ref[0, pl.ds(q0, kwin), cols]
        out = None
        for half in range(2):
            sel = low if half == 0 else jnp.logical_not(low)
            qh = jnp.where(sel, q, jnp.zeros_like(q))
            s = lax.dot_general(
                qh, k, (((1,), (1,)), ((), ())), preferred_element_type=jnp.float32
            ) + bias
            m = jnp.max(s, axis=1, keepdims=True)
            p = jnp.exp(s - m)
            total = jnp.sum(p, axis=1, keepdims=True)
            pv = jnp.dot(p.astype(jnp.bfloat16), v, preferred_element_type=jnp.float32)
            pv = pv / total
            out = pv if out is None else jnp.where(low, out, pv)
        o_ref[0, :, cols] = out.astype(o_ref.dtype)


def band_attention(query_enc, keyval, full_bias):
    spec_dev, bin_dev, width = query_enc.shape
    key_span = keyval.shape[1]
    groups = width // HGROUP
    qblocks = bin_dev // QBLOCK
    kwin = QBLOCK + WINDOW
    return pl.pallas_call(
        band_kernel,
        out_shape=jax.ShapeDtypeStruct(query_enc.shape, jnp.bfloat16),
        grid=(spec_dev, groups, qblocks),
        in_specs=[
            pl.BlockSpec((1, QBLOCK, HGROUP), lambda s, g, b: (s, b, g)),
            pl.BlockSpec((1, key_span, HGROUP), lambda s, g, b: (s, 0, g)),
            pl.BlockSpec((1, key_span, HGROUP), lambda s, g, b: (s, 0, groups + g)),
            pl.BlockSpec((1, 1, QBLOCK, kwin), lambda s, g, b: (s, b, 0, 0)),
        ],
        out_specs=pl.BlockSpec((1, QBLOCK, HGROUP), lambda s, g, b: (s, b, g)),
        compiler_params=pltpu.CompilerParams(
            dimension_semantics=("arbitrary", "arbitrary", "arbitrary")
        ),
        cost_estimate=pl.CostEstimate(
            flops=spec_dev * bin_dev * kwin * width * 8,
            transcendentals=spec_dev * bin_dev * kwin * HE,
            bytes_accessed=spec_dev * (bin_dev * width * 4 + key_span * width * 4)
            + full_bias.size * 4,
        ),
    )(query_enc, keyval, keyval, full_bias)


def cross_kernel(q_ref, k_ref, v_ref, b_ref, o_ref):
    s = lax.dot_general(
        q_ref[0], k_ref[0], (((1,), (1,)), ((), ())), preferred_element_type=jnp.float32
    )
    s = s * DEC_SCALE + b_ref[0]
    m = jnp.max(s, axis=1, keepdims=True)
    p = jnp.exp(s - m)
    total = jnp.sum(p, axis=1, keepdims=True)
    pv = jnp.dot(p.astype(jnp.bfloat16), v_ref[0], preferred_element_type=jnp.float32)
    o_ref[0] = (pv / total).astype(o_ref.dtype)


def cross_attention(query_one, received, mem_bias, heads_here, dec_head):
    _, all_tok, width = query_one.shape
    mem_len = received.shape[1]
    return pl.pallas_call(
        cross_kernel,
        out_shape=jax.ShapeDtypeStruct(query_one.shape, jnp.bfloat16),
        grid=(heads_here,),
        in_specs=[
            pl.BlockSpec((1, all_tok, dec_head), lambda h: (0, 0, h)),
            pl.BlockSpec((1, mem_len, dec_head), lambda h: (0, 0, h)),
            pl.BlockSpec((1, mem_len, dec_head), lambda h: (0, 0, heads_here + h)),
            pl.BlockSpec((1, 1, mem_len), lambda h: (0, 0, 0)),
        ],
        out_specs=pl.BlockSpec((1, all_tok, dec_head), lambda h: (0, 0, h)),
        cost_estimate=pl.CostEstimate(
            flops=all_tok * mem_len * width * 4,
            transcendentals=all_tok * mem_len * heads_here,
            bytes_accessed=all_tok * width * 4 + mem_len * width * 4,
        ),
    )(query_one, received, received, mem_bias)


def per_device(
    spectra,
    key_bias,
    valid_bins,
    enc_query,
    enc_key,
    enc_value,
    enc_out,
    token_ids,
    embedding,
    dec_query,
    mem_key,
    mem_value,
    dec_out,
):
    seq_pos = lax.axis_index("seq")
    head_pos = lax.axis_index("head")
    spec_dev, bin_dev, model_width = spectra.shape
    half_span = WINDOW // 2
    first_spec = head_pos * spec_dev
    first_bin = seq_pos * bin_dev
    my_counts = lax.dynamic_slice_in_dim(valid_bins, first_spec, spec_dev, 0)
    bias_pad = jnp.pad(key_bias, ((0, 0), (half_span, half_span)))
    my_bias = lax.dynamic_slice(
        bias_pad, (first_spec, first_bin), (spec_dev, bin_dev + 2 * half_span)
    )
    kv_weights = jnp.concatenate([enc_key, enc_value], axis=1)

    count = lax.axis_size("seq")
    forward = [(i, i + 1) for i in range(count - 1)]
    backward = [(target, source) for source, target in forward]
    low_edge = lax.ppermute(spectra[:, bin_dev - half_span :], "seq", forward)
    high_edge = lax.ppermute(spectra[:, :half_span], "seq", backward)

    normed = rms_rows(spectra)
    query_enc = jnp.einsum(
        "sbd,de->sbe", normed, enc_query, preferred_element_type=jnp.float32
    ).astype(jnp.bfloat16)
    keyval_mid = jnp.einsum(
        "sbd,de->sbe", normed, kv_weights, preferred_element_type=jnp.float32
    ).astype(jnp.bfloat16)
    edges = rms_rows(jnp.concatenate([low_edge, high_edge], axis=1))
    keyval_edges = jnp.einsum(
        "sbd,de->sbe", edges, kv_weights, preferred_element_type=jnp.float32
    ).astype(jnp.bfloat16)
    keyval = jnp.concatenate(
        [keyval_edges[:, :half_span], keyval_mid, keyval_edges[:, half_span:]], axis=1
    )
    key_span = bin_dev + 2 * half_span
    kwin = QBLOCK + WINDOW
    key_cols = first_bin - half_span + jnp.arange(key_span, dtype=jnp.int32)
    col_ok = (key_cols[None, :] >= 0) & (key_cols[None, :] < my_counts[:, None])
    col_bias = jnp.where(col_ok, my_bias, masked_score)
    windows = jnp.stack(
        [col_bias[:, b * QBLOCK : b * QBLOCK + kwin] for b in range(bin_dev // QBLOCK)], axis=1
    )
    offset = (
        jnp.arange(kwin, dtype=jnp.int32)[None, :] - jnp.arange(QBLOCK, dtype=jnp.int32)[:, None]
    )
    band = (offset >= 0) & (offset <= WINDOW)
    full_bias = jnp.where(band[None, None], windows[:, :, None, :], masked_score)
    context = band_attention(query_enc, keyval, full_bias)

    query_rows = first_bin + jnp.arange(bin_dev, dtype=jnp.int32)
    attended = jnp.einsum("sbd,de->sbe", context, enc_out, preferred_element_type=jnp.float32)
    valid_rows = (query_rows[None, :] < my_counts[:, None])[:, :, None]
    encoded = jnp.where(valid_rows, spectra.astype(jnp.float32) + attended, 0.0).astype(
        jnp.bfloat16
    )
    pooled = jnp.mean(
        encoded.astype(jnp.float32).reshape(spec_dev, bin_dev // POOL, POOL, model_width), axis=2
    ).astype(jnp.bfloat16)
    spectra_all = lax.all_gather(pooled, "head", axis=0, tiled=True)
    mem_weights = jnp.concatenate([mem_key, mem_value], axis=1)
    local_width = mem_key.shape[1]
    memory_part = jnp.einsum(
        "spd,de->spe", rms_rows(spectra_all), mem_weights, preferred_element_type=jnp.float32
    ).astype(jnp.bfloat16)
    spec_count, part_len, part_width = memory_part.shape
    tok_count = token_ids.shape[1]
    id_cols = jnp.zeros((spec_count, part_len, 128), jnp.bfloat16)
    id_cols = id_cols.at[:, 0, :tok_count].set(token_ids.astype(jnp.bfloat16))
    payload = jnp.concatenate([memory_part, id_cols], axis=2)
    received = lax.all_to_all(payload, "seq", 0, 1, tiled=True)
    seq_count = lax.axis_size("seq")
    memory = received[:, :, :part_width]
    ids_one = received.reshape(seq_count, part_len, part_width + 128)[:, 0, part_width : part_width + tok_count]
    ids_one = ids_one.reshape(1, seq_count * tok_count).astype(jnp.int32)
    mem_len = memory.shape[1]
    bias_row = lax.dynamic_slice_in_dim(key_bias, seq_pos, 1, 0)
    pooled_bias = jnp.max(bias_row.reshape(1, mem_len, POOL), axis=2)
    count_row = lax.dynamic_slice_in_dim(valid_bins, seq_pos, 1, 0)
    mem_valid = jnp.arange(mem_len, dtype=jnp.int32)[None, :] * POOL < count_row[:, None]
    dec_width = embedding.shape[1]
    dec_head = dec_width // HD
    heads_here = local_width // dec_head
    share_width = dec_width // lax.axis_size("head")
    vocab = embedding.shape[0]
    onehot = (
        token_ids[:, :, None] == jnp.arange(vocab, dtype=jnp.int32)[None, None, :]
    ).astype(jnp.bfloat16)
    own_table = lax.dynamic_slice_in_dim(embedding, head_pos * share_width, share_width, 1)
    own_part = jnp.einsum(
        "stv,vd->std", onehot, own_table, preferred_element_type=jnp.float32
    ).astype(jnp.bfloat16)
    onehot_one = (
        ids_one[:, :, None] == jnp.arange(vocab, dtype=jnp.int32)[None, None, :]
    ).astype(jnp.bfloat16)
    query_table = jnp.einsum(
        "vd,de->ve", rms_rows(embedding), dec_query, preferred_element_type=jnp.float32
    ).astype(jnp.bfloat16)
    query_one = jnp.einsum(
        "stv,ve->ste", onehot_one, query_table, preferred_element_type=jnp.float32
    ).astype(jnp.bfloat16)
    mem_bias = jnp.where(mem_valid, pooled_bias, masked_score)[:, None, :]
    context_one = cross_attention(query_one, received, mem_bias, heads_here, dec_head)
    dec_context = lax.all_to_all(context_one, "seq", 1, 0, tiled=True)
    partial_sums = jnp.einsum(
        "ste,ed->std", dec_context, dec_out, preferred_element_type=jnp.float32
    )
    summed = lax.psum_scatter(
        partial_sums.astype(jnp.bfloat16), "head", scatter_dimension=2, tiled=True
    ).astype(jnp.float32)
    decoded = (own_part.astype(jnp.float32) + summed).astype(jnp.bfloat16)
    return (encoded, decoded)


def solution(mesh):
    return jax.shard_map(
        per_device,
        mesh=mesh,
        in_specs=(
            P("head", "seq", None),
            P(),
            P(),
            P(),
            P(),
            P(),
            P(),
            P(None, "seq"),
            P(),
            P(None, "head"),
            P(None, "head"),
            P(None, "head"),
            P("head", None),
        ),
        out_specs=(P("head", "seq", None), P(None, "seq", "head")),
        check_vma=False,
    )
```

```python
import jax
import jax.numpy as jnp
from jax import lax
from jax.experimental import pallas as pl
from jax.experimental.pallas import tpu as pltpu
from jax.sharding import PartitionSpec as P

HE = 16
WINDOW = 512
POOL = 32
HD = 32
QBLOCK = 256
HGROUP = 512
DEC_SCALE = 128 ** (-0.5)


epsilon = 1e-05
masked_score = -1e30


def rms_rows(values_in):
    widened = values_in.astype(jnp.float32)
    inverse_rms = lax.rsqrt(jnp.mean(widened * widened, axis=-1, keepdims=True) + epsilon)
    return (widened * inverse_rms).astype(jnp.bfloat16)


def softmax_rows(scores):
    row_top = jnp.max(scores, axis=-1, keepdims=True)
    weights = jnp.exp(scores - row_top)
    return (weights / jnp.sum(weights, axis=-1, keepdims=True)).astype(jnp.bfloat16)


def band_kernel(q_ref, k_ref, v_ref, b_ref, o_ref):
    qb = pl.program_id(2)
    q0 = pl.multiple_of(qb * QBLOCK, QBLOCK)
    kwin = QBLOCK + WINDOW
    bias = b_ref[0, 0]
    lane = lax.broadcasted_iota(jnp.int32, (1, 128), 1)
    low = lane < 64
    for pair in range(HGROUP // 128):
        cols = slice(pair * 128, (pair + 1) * 128)
        q = q_ref[0, :, cols] * 0.125
        k = k_ref[0, pl.ds(q0, kwin), cols]
        v = v_ref[0, pl.ds(q0, kwin), cols]
        out = None
        for half in range(2):
            sel = low if half == 0 else jnp.logical_not(low)
            qh = jnp.where(sel, q, jnp.zeros_like(q))
            s = lax.dot_general(
                qh, k, (((1,), (1,)), ((), ())), preferred_element_type=jnp.float32
            ) + bias
            m = jnp.max(s, axis=1, keepdims=True)
            p = jnp.exp(s - m)
            total = jnp.sum(p, axis=1, keepdims=True)
            pv = jnp.dot(p.astype(jnp.bfloat16), v, preferred_element_type=jnp.float32)
            pv = pv / total
            out = pv if out is None else jnp.where(low, out, pv)
        o_ref[0, :, cols] = out.astype(o_ref.dtype)


def band_attention(query_enc, keyval, full_bias):
    spec_dev, bin_dev, width = query_enc.shape
    key_span = keyval.shape[1]
    groups = width // HGROUP
    qblocks = bin_dev // QBLOCK
    kwin = QBLOCK + WINDOW
    return pl.pallas_call(
        band_kernel,
        out_shape=jax.ShapeDtypeStruct(query_enc.shape, jnp.bfloat16),
        grid=(spec_dev, groups, qblocks),
        in_specs=[
            pl.BlockSpec((1, QBLOCK, HGROUP), lambda s, g, b: (s, b, g)),
            pl.BlockSpec((1, key_span, HGROUP), lambda s, g, b: (s, 0, g)),
            pl.BlockSpec((1, key_span, HGROUP), lambda s, g, b: (s, 0, groups + g)),
            pl.BlockSpec((1, 1, QBLOCK, kwin), lambda s, g, b: (s, b, 0, 0)),
        ],
        out_specs=pl.BlockSpec((1, QBLOCK, HGROUP), lambda s, g, b: (s, b, g)),
        compiler_params=pltpu.CompilerParams(
            dimension_semantics=("arbitrary", "arbitrary", "arbitrary")
        ),
        cost_estimate=pl.CostEstimate(
            flops=spec_dev * bin_dev * kwin * width * 8,
            transcendentals=spec_dev * bin_dev * kwin * HE,
            bytes_accessed=spec_dev * (bin_dev * width * 4 + key_span * width * 4)
            + full_bias.size * 4,
        ),
    )(query_enc, keyval, keyval, full_bias)


def cross_kernel(q_ref, k_ref, v_ref, b_ref, o_ref):
    s = lax.dot_general(
        q_ref[0], k_ref[0], (((1,), (1,)), ((), ())), preferred_element_type=jnp.float32
    )
    s = s * DEC_SCALE + b_ref[0]
    m = jnp.max(s, axis=1, keepdims=True)
    p = jnp.exp(s - m)
    total = jnp.sum(p, axis=1, keepdims=True)
    pv = jnp.dot(p.astype(jnp.bfloat16), v_ref[0], preferred_element_type=jnp.float32)
    o_ref[0] = (pv / total).astype(o_ref.dtype)


def cross_attention(query_one, received, mem_bias, heads_here, dec_head):
    _, all_tok, width = query_one.shape
    mem_len = received.shape[1]
    return pl.pallas_call(
        cross_kernel,
        out_shape=jax.ShapeDtypeStruct(query_one.shape, jnp.bfloat16),
        grid=(heads_here,),
        in_specs=[
            pl.BlockSpec((1, all_tok, dec_head), lambda h: (0, 0, h)),
            pl.BlockSpec((1, mem_len, dec_head), lambda h: (0, 0, h)),
            pl.BlockSpec((1, mem_len, dec_head), lambda h: (0, 0, heads_here + h)),
            pl.BlockSpec((1, 1, mem_len), lambda h: (0, 0, 0)),
        ],
        out_specs=pl.BlockSpec((1, all_tok, dec_head), lambda h: (0, 0, h)),
        cost_estimate=pl.CostEstimate(
            flops=all_tok * mem_len * width * 4,
            transcendentals=all_tok * mem_len * heads_here,
            bytes_accessed=all_tok * width * 4 + mem_len * width * 4,
        ),
    )(query_one, received, received, mem_bias)


def per_device(
    spectra,
    key_bias,
    valid_bins,
    enc_query,
    enc_key,
    enc_value,
    enc_out,
    token_ids,
    embedding,
    dec_query,
    mem_key,
    mem_value,
    dec_out,
):
    seq_pos = lax.axis_index("seq")
    head_pos = lax.axis_index("head")
    spec_dev, bin_dev, model_width = spectra.shape
    half_span = WINDOW // 2
    first_spec = head_pos * spec_dev
    first_bin = seq_pos * bin_dev
    my_counts = lax.dynamic_slice_in_dim(valid_bins, first_spec, spec_dev, 0)
    bias_pad = jnp.pad(key_bias, ((0, 0), (half_span, half_span)))
    my_bias = lax.dynamic_slice(
        bias_pad, (first_spec, first_bin), (spec_dev, bin_dev + 2 * half_span)
    )
    kv_weights = jnp.concatenate([enc_key, enc_value], axis=1)

    count = lax.axis_size("seq")
    forward = [(i, i + 1) for i in range(count - 1)]
    backward = [(target, source) for source, target in forward]
    low_edge = lax.ppermute(spectra[:, bin_dev - half_span :], "seq", forward)
    high_edge = lax.ppermute(spectra[:, :half_span], "seq", backward)

    normed = rms_rows(spectra)
    query_enc = jnp.einsum(
        "sbd,de->sbe", normed, enc_query, preferred_element_type=jnp.float32
    ).astype(jnp.bfloat16)
    keyval_mid = jnp.einsum(
        "sbd,de->sbe", normed, kv_weights, preferred_element_type=jnp.float32
    ).astype(jnp.bfloat16)
    edges = rms_rows(jnp.concatenate([low_edge, high_edge], axis=1))
    keyval_edges = jnp.einsum(
        "sbd,de->sbe", edges, kv_weights, preferred_element_type=jnp.float32
    ).astype(jnp.bfloat16)
    keyval = jnp.concatenate(
        [keyval_edges[:, :half_span], keyval_mid, keyval_edges[:, half_span:]], axis=1
    )
    key_span = bin_dev + 2 * half_span
    kwin = QBLOCK + WINDOW
    key_cols = first_bin - half_span + jnp.arange(key_span, dtype=jnp.int32)
    col_ok = (key_cols[None, :] >= 0) & (key_cols[None, :] < my_counts[:, None])
    col_bias = jnp.where(col_ok, my_bias, masked_score)
    windows = jnp.stack(
        [col_bias[:, b * QBLOCK : b * QBLOCK + kwin] for b in range(bin_dev // QBLOCK)], axis=1
    )
    offset = (
        jnp.arange(kwin, dtype=jnp.int32)[None, :] - jnp.arange(QBLOCK, dtype=jnp.int32)[:, None]
    )
    band = (offset >= 0) & (offset <= WINDOW)
    full_bias = jnp.where(band[None, None], windows[:, :, None, :], masked_score)
    context = band_attention(query_enc, keyval, full_bias)

    query_rows = first_bin + jnp.arange(bin_dev, dtype=jnp.int32)
    attended = jnp.einsum("sbd,de->sbe", context, enc_out, preferred_element_type=jnp.float32)
    valid_rows = (query_rows[None, :] < my_counts[:, None])[:, :, None]
    encoded = jnp.where(valid_rows, spectra.astype(jnp.float32) + attended, 0.0).astype(
        jnp.bfloat16
    )
    pooled = jnp.mean(
        encoded.astype(jnp.float32).reshape(spec_dev, bin_dev // POOL, POOL, model_width), axis=2
    ).astype(jnp.bfloat16)
    spectra_all = lax.all_gather(pooled, "head", axis=0, tiled=True)
    mem_weights = jnp.concatenate([mem_key, mem_value], axis=1)
    local_width = mem_key.shape[1]
    memory_part = jnp.einsum(
        "spd,de->spe", rms_rows(spectra_all), mem_weights, preferred_element_type=jnp.float32
    ).astype(jnp.bfloat16)
    spec_count, part_len, part_width = memory_part.shape
    tok_count = token_ids.shape[1]
    id_cols = jnp.zeros((spec_count, part_len, 128), jnp.bfloat16)
    id_cols = id_cols.at[:, 0, :tok_count].set(token_ids.astype(jnp.bfloat16))
    payload = jnp.concatenate([memory_part, id_cols], axis=2)
    received = lax.all_to_all(payload, "seq", 0, 1, tiled=True)
    seq_count = lax.axis_size("seq")
    memory = received[:, :, :part_width]
    ids_one = received.reshape(seq_count, part_len, part_width + 128)[:, 0, part_width : part_width + tok_count]
    ids_one = ids_one.reshape(1, seq_count * tok_count).astype(jnp.int32)
    mem_len = memory.shape[1]
    bias_row = lax.dynamic_slice_in_dim(key_bias, seq_pos, 1, 0)
    pooled_bias = jnp.max(bias_row.reshape(1, mem_len, POOL), axis=2)
    count_row = lax.dynamic_slice_in_dim(valid_bins, seq_pos, 1, 0)
    mem_valid = jnp.arange(mem_len, dtype=jnp.int32)[None, :] * POOL < count_row[:, None]
    dec_width = embedding.shape[1]
    dec_head = dec_width // HD
    heads_here = local_width // dec_head
    share_width = dec_width // lax.axis_size("head")
    vocab = embedding.shape[0]
    onehot = (
        token_ids[:, :, None] == jnp.arange(vocab, dtype=jnp.int32)[None, None, :]
    ).astype(jnp.bfloat16)
    own_table = lax.dynamic_slice_in_dim(embedding, head_pos * share_width, share_width, 1)
    own_part = jnp.einsum(
        "stv,vd->std", onehot, own_table, preferred_element_type=jnp.float32
    ).astype(jnp.bfloat16)
    query_table = jnp.einsum(
        "vd,de->ve", rms_rows(embedding), dec_query, preferred_element_type=jnp.float32
    ).astype(jnp.bfloat16)
    query_one = jnp.take(query_table, ids_one[0], axis=0)[None]
    mem_bias = jnp.where(mem_valid, pooled_bias, masked_score)[:, None, :]
    context_one = cross_attention(query_one, received, mem_bias, heads_here, dec_head)
    context_one = context_one.reshape(seq_count, tok_count, local_width)
    dec_context = lax.all_to_all(context_one, "seq", 0, 0, tiled=True)
    partial_sums = jnp.einsum(
        "ste,ed->std", dec_context, dec_out, preferred_element_type=jnp.float32
    )
    summed = lax.psum_scatter(
        partial_sums.astype(jnp.bfloat16), "head", scatter_dimension=2, tiled=True
    ).astype(jnp.float32)
    decoded = (own_part.astype(jnp.float32) + summed).astype(jnp.bfloat16)
    return (encoded, decoded)


def solution(mesh):
    return jax.shard_map(
        per_device,
        mesh=mesh,
        in_specs=(
            P("head", "seq", None),
            P(),
            P(),
            P(),
            P(),
            P(),
            P(),
            P(None, "seq"),
            P(),
            P(None, "head"),
            P(None, "head"),
            P(None, "head"),
            P("head", None),
        ),
        out_specs=(P("head", "seq", None), P(None, "seq", "head")),
        check_vma=False,
    )
```

```python
import jax
import jax.numpy as jnp
from jax import lax
from jax.experimental import pallas as pl
from jax.experimental.pallas import tpu as pltpu
from jax.sharding import PartitionSpec as P

HE = 16
WINDOW = 512
POOL = 32
HD = 32
QBLOCK = 256
HGROUP = 512
DEC_SCALE = 128 ** (-0.5)


epsilon = 1e-05
masked_score = -1e30


def rms_rows(values_in):
    widened = values_in.astype(jnp.float32)
    inverse_rms = lax.rsqrt(jnp.mean(widened * widened, axis=-1, keepdims=True) + epsilon)
    return (widened * inverse_rms).astype(jnp.bfloat16)


def softmax_rows(scores):
    row_top = jnp.max(scores, axis=-1, keepdims=True)
    weights = jnp.exp(scores - row_top)
    return (weights / jnp.sum(weights, axis=-1, keepdims=True)).astype(jnp.bfloat16)


def band_kernel(q_ref, km_ref, vm_ref, ke_ref, ve_ref, bm_ref, be_ref, o_ref):
    bias_mid = bm_ref[0, 0]
    bias_edge = be_ref[0, 0]
    lane = lax.broadcasted_iota(jnp.int32, (1, 128), 1)
    low = lane < 64
    dims = (((1,), (1,)), ((), ()))
    for pair in range(HGROUP // 128):
        cols = slice(pair * 128, (pair + 1) * 128)
        q = q_ref[0, :, cols] * 0.125
        key_mid = km_ref[0, :, cols]
        key_edge = ke_ref[0, :, cols]
        out = None
        for half in range(2):
            sel = low if half == 0 else jnp.logical_not(low)
            qh = jnp.where(sel, q, jnp.zeros_like(q))
            s_mid = lax.dot_general(qh, key_mid, dims, preferred_element_type=jnp.float32)
            s_mid = s_mid + bias_mid
            s_edge = lax.dot_general(qh, key_edge, dims, preferred_element_type=jnp.float32)
            s_edge = s_edge + bias_edge
            m = jnp.maximum(
                jnp.max(s_mid, axis=1, keepdims=True), jnp.max(s_edge, axis=1, keepdims=True)
            )
            p_mid = jnp.exp(s_mid - m)
            p_edge = jnp.exp(s_edge - m)
            total = jnp.sum(p_mid, axis=1, keepdims=True) + jnp.sum(p_edge, axis=1, keepdims=True)
            pv = jnp.dot(
                p_mid.astype(jnp.bfloat16), vm_ref[0, :, cols], preferred_element_type=jnp.float32
            ) + jnp.dot(
                p_edge.astype(jnp.bfloat16), ve_ref[0, :, cols], preferred_element_type=jnp.float32
            )
            pv = pv / total
            out = pv if out is None else jnp.where(low, out, pv)
        o_ref[0, :, cols] = out.astype(o_ref.dtype)


def band_attention(qkv, keyval_edges, bias_mid, bias_edge):
    spec_dev, bin_dev, triple = qkv.shape
    width = triple // 3
    edge_rows = keyval_edges.shape[1] // 2
    groups = width // HGROUP
    qblocks = bin_dev // QBLOCK
    kwin = bin_dev + edge_rows
    return pl.pallas_call(
        band_kernel,
        out_shape=jax.ShapeDtypeStruct((spec_dev, bin_dev, width), jnp.bfloat16),
        grid=(spec_dev, groups, qblocks),
        in_specs=[
            pl.BlockSpec((1, QBLOCK, HGROUP), lambda s, g, b: (s, b, g)),
            pl.BlockSpec((1, bin_dev, HGROUP), lambda s, g, b: (s, 0, groups + g)),
            pl.BlockSpec((1, bin_dev, HGROUP), lambda s, g, b: (s, 0, 2 * groups + g)),
            pl.BlockSpec((1, edge_rows, HGROUP), lambda s, g, b: (s, b, g)),
            pl.BlockSpec((1, edge_rows, HGROUP), lambda s, g, b: (s, b, groups + g)),
            pl.BlockSpec((1, 1, QBLOCK, bin_dev), lambda s, g, b: (s, b, 0, 0)),
            pl.BlockSpec((1, 1, QBLOCK, edge_rows), lambda s, g, b: (s, b, 0, 0)),
        ],
        out_specs=pl.BlockSpec((1, QBLOCK, HGROUP), lambda s, g, b: (s, b, g)),
        compiler_params=pltpu.CompilerParams(
            dimension_semantics=("arbitrary", "arbitrary", "arbitrary")
        ),
        cost_estimate=pl.CostEstimate(
            flops=spec_dev * bin_dev * kwin * width * 8,
            transcendentals=spec_dev * bin_dev * kwin * HE,
            bytes_accessed=spec_dev * bin_dev * width * 10
            + (bias_mid.size + bias_edge.size) * 4,
        ),
    )(qkv, qkv, qkv, keyval_edges, keyval_edges, bias_mid, bias_edge)


def cross_kernel(q_ref, k_ref, v_ref, b_ref, o_ref):
    s = lax.dot_general(
        q_ref[0], k_ref[0], (((1,), (1,)), ((), ())), preferred_element_type=jnp.float32
    )
    s = s * DEC_SCALE + b_ref[0]
    m = jnp.max(s, axis=1, keepdims=True)
    p = jnp.exp(s - m)
    total = jnp.sum(p, axis=1, keepdims=True)
    pv = jnp.dot(p.astype(jnp.bfloat16), v_ref[0], preferred_element_type=jnp.float32)
    o_ref[0] = (pv / total).astype(o_ref.dtype)


def cross_attention(query_one, received, mem_bias, heads_here, dec_head):
    _, all_tok, width = query_one.shape
    mem_len = received.shape[1]
    return pl.pallas_call(
        cross_kernel,
        out_shape=jax.ShapeDtypeStruct(query_one.shape, jnp.bfloat16),
        grid=(heads_here,),
        in_specs=[
            pl.BlockSpec((1, all_tok, dec_head), lambda h: (0, 0, h)),
            pl.BlockSpec((1, mem_len, dec_head), lambda h: (0, 0, h)),
            pl.BlockSpec((1, mem_len, dec_head), lambda h: (0, 0, heads_here + h)),
            pl.BlockSpec((1, 1, mem_len), lambda h: (0, 0, 0)),
        ],
        out_specs=pl.BlockSpec((1, all_tok, dec_head), lambda h: (0, 0, h)),
        cost_estimate=pl.CostEstimate(
            flops=all_tok * mem_len * width * 4,
            transcendentals=all_tok * mem_len * heads_here,
            bytes_accessed=all_tok * width * 4 + mem_len * width * 4,
        ),
    )(query_one, received, received, mem_bias)


def per_device(
    spectra,
    key_bias,
    valid_bins,
    enc_query,
    enc_key,
    enc_value,
    enc_out,
    token_ids,
    embedding,
    dec_query,
    mem_key,
    mem_value,
    dec_out,
):
    seq_pos = lax.axis_index("seq")
    head_pos = lax.axis_index("head")
    spec_dev, bin_dev, model_width = spectra.shape
    half_span = WINDOW // 2
    first_spec = head_pos * spec_dev
    first_bin = seq_pos * bin_dev
    my_counts = lax.dynamic_slice_in_dim(valid_bins, first_spec, spec_dev, 0)
    bias_pad = jnp.pad(key_bias, ((0, 0), (half_span, half_span)))
    my_bias = lax.dynamic_slice(
        bias_pad, (first_spec, first_bin), (spec_dev, bin_dev + 2 * half_span)
    )
    kv_weights = jnp.concatenate([enc_key, enc_value], axis=1)
    qkv_weights = jnp.concatenate([enc_query, enc_key, enc_value], axis=1)

    count = lax.axis_size("seq")
    forward = [(i, i + 1) for i in range(count - 1)]
    backward = [(target, source) for source, target in forward]
    low_edge = lax.ppermute(spectra[:, bin_dev - half_span :], "seq", forward)
    high_edge = lax.ppermute(spectra[:, :half_span], "seq", backward)

    normed = rms_rows(spectra)
    qkv = jnp.einsum(
        "sbd,de->sbe", normed, qkv_weights, preferred_element_type=jnp.float32
    ).astype(jnp.bfloat16)
    edges = rms_rows(jnp.concatenate([low_edge, high_edge], axis=1))
    keyval_edges = jnp.einsum(
        "sbd,de->sbe", edges, kv_weights, preferred_element_type=jnp.float32
    ).astype(jnp.bfloat16)
    key_span = bin_dev + 2 * half_span
    key_cols = first_bin - half_span + jnp.arange(key_span, dtype=jnp.int32)
    col_ok = (key_cols[None, :] >= 0) & (key_cols[None, :] < my_counts[:, None])
    col_bias = jnp.where(col_ok, my_bias, masked_score)
    qblocks = bin_dev // QBLOCK
    block_ix = jnp.arange(qblocks, dtype=jnp.int32)[:, None, None]
    query_local = block_ix * QBLOCK + jnp.arange(QBLOCK, dtype=jnp.int32)[None, :, None]
    key_mid = half_span + jnp.arange(bin_dev, dtype=jnp.int32)[None, None, :]
    key_edge = jnp.arange(half_span, dtype=jnp.int32)[None, None, :] + block_ix * (
        key_span - half_span
    )
    band_mid = (key_mid - query_local >= 0) & (key_mid - query_local <= WINDOW)
    band_edge = (key_edge - query_local >= 0) & (key_edge - query_local <= WINDOW)
    col_mid = col_bias[:, half_span : half_span + bin_dev]
    col_edge = col_bias.reshape(spec_dev, key_span // half_span, half_span)[:, :: qblocks + 1]
    bias_mid = jnp.where(band_mid[None], col_mid[:, None, None, :], masked_score)
    bias_edge = jnp.where(band_edge[None], col_edge[:, :, None, :], masked_score)
    context = band_attention(qkv, keyval_edges, bias_mid, bias_edge)

    query_rows = first_bin + jnp.arange(bin_dev, dtype=jnp.int32)
    attended = jnp.einsum("sbd,de->sbe", context, enc_out, preferred_element_type=jnp.float32)
    valid_rows = (query_rows[None, :] < my_counts[:, None])[:, :, None]
    encoded = jnp.where(valid_rows, spectra.astype(jnp.float32) + attended, 0.0).astype(
        jnp.bfloat16
    )
    pooled = jnp.mean(
        encoded.astype(jnp.float32).reshape(spec_dev, bin_dev // POOL, POOL, model_width), axis=2
    ).astype(jnp.bfloat16)
    spectra_all = lax.all_gather(pooled, "head", axis=0, tiled=True)
    mem_weights = jnp.concatenate([mem_key, mem_value], axis=1)
    local_width = mem_key.shape[1]
    memory_part = jnp.einsum(
        "spd,de->spe", rms_rows(spectra_all), mem_weights, preferred_element_type=jnp.float32
    ).astype(jnp.bfloat16)
    spec_count, part_len, part_width = memory_part.shape
    tok_count = token_ids.shape[1]
    id_cols = jnp.zeros((spec_count, part_len, 128), jnp.bfloat16)
    id_cols = id_cols.at[:, 0, :tok_count].set(token_ids.astype(jnp.bfloat16))
    payload = jnp.concatenate([memory_part, id_cols], axis=2)
    received = lax.all_to_all(payload, "seq", 0, 1, tiled=True)
    seq_count = lax.axis_size("seq")
    memory = received[:, :, :part_width]
    ids_one = received.reshape(seq_count, part_len, part_width + 128)[:, 0, part_width : part_width + tok_count]
    ids_one = ids_one.reshape(1, seq_count * tok_count).astype(jnp.int32)
    mem_len = memory.shape[1]
    bias_row = lax.dynamic_slice_in_dim(key_bias, seq_pos, 1, 0)
    pooled_bias = jnp.max(bias_row.reshape(1, mem_len, POOL), axis=2)
    count_row = lax.dynamic_slice_in_dim(valid_bins, seq_pos, 1, 0)
    mem_valid = jnp.arange(mem_len, dtype=jnp.int32)[None, :] * POOL < count_row[:, None]
    dec_width = embedding.shape[1]
    dec_head = dec_width // HD
    heads_here = local_width // dec_head
    share_width = dec_width // lax.axis_size("head")
    vocab = embedding.shape[0]
    onehot = (
        token_ids[:, :, None] == jnp.arange(vocab, dtype=jnp.int32)[None, None, :]
    ).astype(jnp.bfloat16)
    own_table = lax.dynamic_slice_in_dim(embedding, head_pos * share_width, share_width, 1)
    own_part = jnp.einsum(
        "stv,vd->std", onehot, own_table, preferred_element_type=jnp.float32
    ).astype(jnp.bfloat16)
    query_table = jnp.einsum(
        "vd,de->ve", rms_rows(embedding), dec_query, preferred_element_type=jnp.float32
    ).astype(jnp.bfloat16)
    query_one = jnp.take(query_table, ids_one[0], axis=0)[None]
    mem_bias = jnp.where(mem_valid, pooled_bias, masked_score)[:, None, :]
    context_one = cross_attention(query_one, received, mem_bias, heads_here, dec_head)
    context_one = context_one.reshape(seq_count, tok_count, local_width)
    dec_context = lax.all_to_all(context_one, "seq", 0, 0, tiled=True)
    partial_sums = jnp.einsum(
        "ste,ed->std", dec_context, dec_out, preferred_element_type=jnp.float32
    )
    summed = lax.psum_scatter(
        partial_sums.astype(jnp.bfloat16), "head", scatter_dimension=2, tiled=True
    ).astype(jnp.float32)
    decoded = (own_part.astype(jnp.float32) + summed).astype(jnp.bfloat16)
    return (encoded, decoded)


def solution(mesh):
    return jax.shard_map(
        per_device,
        mesh=mesh,
        in_specs=(
            P("head", "seq", None),
            P(),
            P(),
            P(),
            P(),
            P(),
            P(),
            P(None, "seq"),
            P(),
            P(None, "head"),
            P(None, "head"),
            P(None, "head"),
            P("head", None),
        ),
        out_specs=(P("head", "seq", None), P(None, "seq", "head")),
        check_vma=False,
    )
```

```python
import jax
import jax.numpy as jnp
from jax import lax
from jax.experimental import pallas as pl
from jax.experimental.pallas import tpu as pltpu
from jax.sharding import PartitionSpec as P

HE = 16
WINDOW = 512
POOL = 32
HD = 32
QBLOCK = 256
HGROUP = 1024
DEC_SCALE = 128 ** (-0.5)


epsilon = 1e-05
masked_score = -1e30


def rms_rows(values_in):
    widened = values_in.astype(jnp.float32)
    inverse_rms = lax.rsqrt(jnp.mean(widened * widened, axis=-1, keepdims=True) + epsilon)
    return (widened * inverse_rms).astype(jnp.bfloat16)


def softmax_rows(scores):
    row_top = jnp.max(scores, axis=-1, keepdims=True)
    weights = jnp.exp(scores - row_top)
    return (weights / jnp.sum(weights, axis=-1, keepdims=True)).astype(jnp.bfloat16)


def band_kernel(
    q_ref, km_ref, vm_ref, ke_ref, ve_ref, bm_ref, be_ref, eo_ref, sp_ref, rv_ref, pm_ref,
    e_ref, p_ref, ctx
):
    bias_mid = bm_ref[0, 0]
    bias_edge = be_ref[0, 0]
    lane = lax.broadcasted_iota(jnp.int32, (1, 128), 1)
    low = lane < 64
    dims = (((1,), (1,)), ((), ()))
    for pair in range(HGROUP // 128):
        cols = slice(pair * 128, (pair + 1) * 128)
        q = q_ref[0, :, cols] * 0.125
        key_mid = km_ref[0, :, cols]
        key_edge = ke_ref[0, :, cols]
        out = None
        for half in range(2):
            sel = low if half == 0 else jnp.logical_not(low)
            qh = jnp.where(sel, q, jnp.zeros_like(q))
            s_mid = lax.dot_general(qh, key_mid, dims, preferred_element_type=jnp.float32)
            s_mid = s_mid + bias_mid
            s_edge = lax.dot_general(qh, key_edge, dims, preferred_element_type=jnp.float32)
            s_edge = s_edge + bias_edge
            m = jnp.maximum(
                jnp.max(s_mid, axis=1, keepdims=True), jnp.max(s_edge, axis=1, keepdims=True)
            )
            p_mid = jnp.exp(s_mid - m)
            p_edge = jnp.exp(s_edge - m)
            total = jnp.sum(p_mid, axis=1, keepdims=True) + jnp.sum(p_edge, axis=1, keepdims=True)
            pv = jnp.dot(
                p_mid.astype(jnp.bfloat16), vm_ref[0, :, cols], preferred_element_type=jnp.float32
            ) + jnp.dot(
                p_edge.astype(jnp.bfloat16), ve_ref[0, :, cols], preferred_element_type=jnp.float32
            )
            pv = pv / total
            out = pv if out is None else jnp.where(low, out, pv)
        ctx[:, cols] = out.astype(jnp.bfloat16)
    attended = jnp.dot(ctx[...], eo_ref[...], preferred_element_type=jnp.float32)
    rows = sp_ref[0].astype(jnp.float32) + attended
    encoded = jnp.where(rv_ref[0] > 0, rows, 0.0).astype(jnp.bfloat16)
    e_ref[0] = encoded
    p_ref[0] = jnp.dot(pm_ref[...], encoded, preferred_element_type=jnp.float32)


def band_attention(qkv, keyval_edges, bias_mid, bias_edge, enc_out, spectra, row_valid):
    spec_dev, bin_dev, triple = qkv.shape
    width = triple // 3
    edge_rows = keyval_edges.shape[1] // 2
    groups = width // HGROUP
    qblocks = bin_dev // QBLOCK
    kwin = bin_dev + edge_rows
    pooled_rows = QBLOCK // POOL
    pool_matrix = (
        jnp.arange(QBLOCK, dtype=jnp.int32)[None, :] // POOL
        == jnp.arange(pooled_rows, dtype=jnp.int32)[:, None]
    ).astype(jnp.bfloat16) * (1.0 / POOL)
    return pl.pallas_call(
        band_kernel,
        out_shape=(
            jax.ShapeDtypeStruct((spec_dev, bin_dev, width), jnp.bfloat16),
            jax.ShapeDtypeStruct((spec_dev, bin_dev // POOL, width), jnp.float32),
        ),
        grid=(spec_dev, qblocks),
        in_specs=[
            pl.BlockSpec((1, QBLOCK, HGROUP), lambda s, b: (s, b, 0)),
            pl.BlockSpec((1, bin_dev, HGROUP), lambda s, b: (s, 0, groups)),
            pl.BlockSpec((1, bin_dev, HGROUP), lambda s, b: (s, 0, 2 * groups)),
            pl.BlockSpec((1, edge_rows, HGROUP), lambda s, b: (s, b, 0)),
            pl.BlockSpec((1, edge_rows, HGROUP), lambda s, b: (s, b, groups)),
            pl.BlockSpec((1, 1, QBLOCK, bin_dev), lambda s, b: (s, b, 0, 0)),
            pl.BlockSpec((1, 1, QBLOCK, edge_rows), lambda s, b: (s, b, 0, 0)),
            pl.BlockSpec((width, width), lambda s, b: (0, 0)),
            pl.BlockSpec((1, QBLOCK, width), lambda s, b: (s, b, 0)),
            pl.BlockSpec((1, QBLOCK, 1), lambda s, b: (s, b, 0)),
            pl.BlockSpec((pooled_rows, QBLOCK), lambda s, b: (0, 0)),
        ],
        out_specs=(
            pl.BlockSpec((1, QBLOCK, width), lambda s, b: (s, b, 0)),
            pl.BlockSpec((1, pooled_rows, width), lambda s, b: (s, b, 0)),
        ),
        scratch_shapes=[pltpu.VMEM((QBLOCK, width), jnp.bfloat16)],
        compiler_params=pltpu.CompilerParams(dimension_semantics=("arbitrary", "arbitrary")),
        cost_estimate=pl.CostEstimate(
            flops=spec_dev * bin_dev * (kwin * width * 8 + width * width * 2),
            transcendentals=spec_dev * bin_dev * kwin * HE,
            bytes_accessed=spec_dev * bin_dev * width * 14
            + (bias_mid.size + bias_edge.size) * 4
            + width * width * 2,
        ),
    )(
        qkv, qkv, qkv, keyval_edges, keyval_edges, bias_mid, bias_edge,
        enc_out, spectra, row_valid, pool_matrix,
    )

def cross_kernel(q_ref, k_ref, v_ref, b_ref, o_ref):
    s = lax.dot_general(
        q_ref[0], k_ref[0], (((1,), (1,)), ((), ())), preferred_element_type=jnp.float32
    )
    s = s * DEC_SCALE + b_ref[0]
    m = jnp.max(s, axis=1, keepdims=True)
    p = jnp.exp(s - m)
    total = jnp.sum(p, axis=1, keepdims=True)
    pv = jnp.dot(p.astype(jnp.bfloat16), v_ref[0], preferred_element_type=jnp.float32)
    o_ref[0] = (pv / total).astype(o_ref.dtype)


def cross_attention(query_one, received, mem_bias, heads_here, dec_head):
    _, all_tok, width = query_one.shape
    mem_len = received.shape[1]
    return pl.pallas_call(
        cross_kernel,
        out_shape=jax.ShapeDtypeStruct(query_one.shape, jnp.bfloat16),
        grid=(heads_here,),
        in_specs=[
            pl.BlockSpec((1, all_tok, dec_head), lambda h: (0, 0, h)),
            pl.BlockSpec((1, mem_len, dec_head), lambda h: (0, 0, h)),
            pl.BlockSpec((1, mem_len, dec_head), lambda h: (0, 0, heads_here + h)),
            pl.BlockSpec((1, 1, mem_len), lambda h: (0, 0, 0)),
        ],
        out_specs=pl.BlockSpec((1, all_tok, dec_head), lambda h: (0, 0, h)),
        cost_estimate=pl.CostEstimate(
            flops=all_tok * mem_len * width * 4,
            transcendentals=all_tok * mem_len * heads_here,
            bytes_accessed=all_tok * width * 4 + mem_len * width * 4,
        ),
    )(query_one, received, received, mem_bias)


def per_device(
    spectra,
    key_bias,
    valid_bins,
    enc_query,
    enc_key,
    enc_value,
    enc_out,
    token_ids,
    embedding,
    dec_query,
    mem_key,
    mem_value,
    dec_out,
):
    seq_pos = lax.axis_index("seq")
    head_pos = lax.axis_index("head")
    spec_dev, bin_dev, model_width = spectra.shape
    half_span = WINDOW // 2
    first_spec = head_pos * spec_dev
    first_bin = seq_pos * bin_dev
    my_counts = lax.dynamic_slice_in_dim(valid_bins, first_spec, spec_dev, 0)
    bias_pad = jnp.pad(key_bias, ((0, 0), (half_span, half_span)))
    my_bias = lax.dynamic_slice(
        bias_pad, (first_spec, first_bin), (spec_dev, bin_dev + 2 * half_span)
    )
    kv_weights = jnp.concatenate([enc_key, enc_value], axis=1)
    qkv_weights = jnp.concatenate([enc_query, enc_key, enc_value], axis=1)

    count = lax.axis_size("seq")
    forward = [(i, i + 1) for i in range(count - 1)]
    backward = [(target, source) for source, target in forward]
    low_edge = lax.ppermute(spectra[:, bin_dev - half_span :], "seq", forward)
    high_edge = lax.ppermute(spectra[:, :half_span], "seq", backward)

    normed = rms_rows(spectra)
    qkv = jnp.einsum(
        "sbd,de->sbe", normed, qkv_weights, preferred_element_type=jnp.float32
    ).astype(jnp.bfloat16)
    edges = rms_rows(jnp.concatenate([low_edge, high_edge], axis=1))
    keyval_edges = jnp.einsum(
        "sbd,de->sbe", edges, kv_weights, preferred_element_type=jnp.float32
    ).astype(jnp.bfloat16)
    key_span = bin_dev + 2 * half_span
    key_cols = first_bin - half_span + jnp.arange(key_span, dtype=jnp.int32)
    col_ok = (key_cols[None, :] >= 0) & (key_cols[None, :] < my_counts[:, None])
    col_bias = jnp.where(col_ok, my_bias, masked_score)
    qblocks = bin_dev // QBLOCK
    block_ix = jnp.arange(qblocks, dtype=jnp.int32)[:, None, None]
    query_local = block_ix * QBLOCK + jnp.arange(QBLOCK, dtype=jnp.int32)[None, :, None]
    key_mid = half_span + jnp.arange(bin_dev, dtype=jnp.int32)[None, None, :]
    key_edge = jnp.arange(half_span, dtype=jnp.int32)[None, None, :] + block_ix * (
        key_span - half_span
    )
    band_mid = (key_mid - query_local >= 0) & (key_mid - query_local <= WINDOW)
    band_edge = (key_edge - query_local >= 0) & (key_edge - query_local <= WINDOW)
    col_mid = col_bias[:, half_span : half_span + bin_dev]
    col_edge = col_bias.reshape(spec_dev, key_span // half_span, half_span)[:, :: qblocks + 1]
    bias_mid = jnp.where(band_mid[None], col_mid[:, None, None, :], masked_score)
    bias_edge = jnp.where(band_edge[None], col_edge[:, :, None, :], masked_score)
    query_rows = first_bin + jnp.arange(bin_dev, dtype=jnp.int32)
    row_valid = (query_rows[None, :] < my_counts[:, None]).astype(jnp.int32)[:, :, None]
    encoded, pooled_sums = band_attention(
        qkv, keyval_edges, bias_mid, bias_edge, enc_out, spectra, row_valid
    )
    pooled = pooled_sums.astype(jnp.bfloat16)
    spectra_all = lax.all_gather(pooled, "head", axis=0, tiled=True)
    mem_weights = jnp.concatenate([mem_key, mem_value], axis=1)
    local_width = mem_key.shape[1]
    memory_part = jnp.einsum(
        "spd,de->spe", rms_rows(spectra_all), mem_weights, preferred_element_type=jnp.float32
    ).astype(jnp.bfloat16)
    spec_count, part_len, part_width = memory_part.shape
    tok_count = token_ids.shape[1]
    id_cols = jnp.zeros((spec_count, part_len, 128), jnp.bfloat16)
    id_cols = id_cols.at[:, 0, :tok_count].set(token_ids.astype(jnp.bfloat16))
    payload = jnp.concatenate([memory_part, id_cols], axis=2)
    received = lax.all_to_all(payload, "seq", 0, 1, tiled=True)
    seq_count = lax.axis_size("seq")
    memory = received[:, :, :part_width]
    ids_one = received.reshape(seq_count, part_len, part_width + 128)[:, 0, part_width : part_width + tok_count]
    ids_one = ids_one.reshape(1, seq_count * tok_count).astype(jnp.int32)
    mem_len = memory.shape[1]
    bias_row = lax.dynamic_slice_in_dim(key_bias, seq_pos, 1, 0)
    pooled_bias = jnp.max(bias_row.reshape(1, mem_len, POOL), axis=2)
    count_row = lax.dynamic_slice_in_dim(valid_bins, seq_pos, 1, 0)
    mem_valid = jnp.arange(mem_len, dtype=jnp.int32)[None, :] * POOL < count_row[:, None]
    dec_width = embedding.shape[1]
    dec_head = dec_width // HD
    heads_here = local_width // dec_head
    share_width = dec_width // lax.axis_size("head")
    vocab = embedding.shape[0]
    onehot = (
        token_ids[:, :, None] == jnp.arange(vocab, dtype=jnp.int32)[None, None, :]
    ).astype(jnp.bfloat16)
    own_table = lax.dynamic_slice_in_dim(embedding, head_pos * share_width, share_width, 1)
    own_part = jnp.einsum(
        "stv,vd->std", onehot, own_table, preferred_element_type=jnp.float32
    ).astype(jnp.bfloat16)
    query_table = jnp.einsum(
        "vd,de->ve", rms_rows(embedding), dec_query, preferred_element_type=jnp.float32
    ).astype(jnp.bfloat16)
    query_one = jnp.take(query_table, ids_one[0], axis=0)[None]
    mem_bias = jnp.where(mem_valid, pooled_bias, masked_score)[:, None, :]
    context_one = cross_attention(query_one, received, mem_bias, heads_here, dec_head)
    context_one = context_one.reshape(seq_count, tok_count, local_width)
    dec_context = lax.all_to_all(context_one, "seq", 0, 0, tiled=True)
    partial_sums = jnp.einsum(
        "ste,ed->std", dec_context, dec_out, preferred_element_type=jnp.float32
    )
    summed = lax.psum_scatter(
        partial_sums.astype(jnp.bfloat16), "head", scatter_dimension=2, tiled=True
    ).astype(jnp.float32)
    decoded = (own_part.astype(jnp.float32) + summed).astype(jnp.bfloat16)
    return (encoded, decoded)


def solution(mesh):
    return jax.shard_map(
        per_device,
        mesh=mesh,
        in_specs=(
            P("head", "seq", None),
            P(),
            P(),
            P(),
            P(),
            P(),
            P(),
            P(None, "seq"),
            P(),
            P(None, "head"),
            P(None, "head"),
            P(None, "head"),
            P("head", None),
        ),
        out_specs=(P("head", "seq", None), P(None, "seq", "head")),
        check_vma=False,
    )
```

```python
import jax
import jax.numpy as jnp
from jax import lax
from jax.experimental import pallas as pl
from jax.experimental.pallas import tpu as pltpu
from jax.sharding import PartitionSpec as P

HE = 16
WINDOW = 512
POOL = 32
HD = 32
QBLOCK = 256
HGROUP = 1024
DEC_SCALE = 128 ** (-0.5)


epsilon = 1e-05
masked_score = -1e30


def rms_rows(values_in):
    widened = values_in.astype(jnp.float32)
    inverse_rms = lax.rsqrt(jnp.mean(widened * widened, axis=-1, keepdims=True) + epsilon)
    return (widened * inverse_rms).astype(jnp.bfloat16)


def softmax_rows(scores):
    row_top = jnp.max(scores, axis=-1, keepdims=True)
    weights = jnp.exp(scores - row_top)
    return (weights / jnp.sum(weights, axis=-1, keepdims=True)).astype(jnp.bfloat16)


def band_kernel(
    q_ref, km_ref, vm_ref, ke_ref, ve_ref, bm_ref, be_ref, eo_ref, sp_ref, lim_ref, e_ref, p_ref, ctx
):
    bias_mid = bm_ref[0, 0]
    bias_edge = be_ref[0, 0]
    lane = lax.broadcasted_iota(jnp.int32, (1, 128), 1)
    low = lane < 64
    dims = (((1,), (1,)), ((), ()))
    for pair in range(HGROUP // 128):
        cols = slice(pair * 128, (pair + 1) * 128)
        q = q_ref[0, :, cols] * 0.125
        key_mid = km_ref[0, :, cols]
        key_edge = ke_ref[0, :, cols]
        out = None
        for half in range(2):
            sel = low if half == 0 else jnp.logical_not(low)
            qh = jnp.where(sel, q, jnp.zeros_like(q))
            s_mid = lax.dot_general(qh, key_mid, dims, preferred_element_type=jnp.float32)
            s_mid = s_mid + bias_mid
            s_edge = lax.dot_general(qh, key_edge, dims, preferred_element_type=jnp.float32)
            s_edge = s_edge + bias_edge
            m = jnp.maximum(
                jnp.max(s_mid, axis=1, keepdims=True), jnp.max(s_edge, axis=1, keepdims=True)
            )
            p_mid = jnp.exp(s_mid - m)
            p_edge = jnp.exp(s_edge - m)
            total = jnp.sum(p_mid, axis=1, keepdims=True) + jnp.sum(p_edge, axis=1, keepdims=True)
            pv = jnp.dot(
                p_mid.astype(jnp.bfloat16), vm_ref[0, :, cols], preferred_element_type=jnp.float32
            ) + jnp.dot(
                p_edge.astype(jnp.bfloat16), ve_ref[0, :, cols], preferred_element_type=jnp.float32
            )
            pv = pv / total
            out = pv if out is None else jnp.where(low, out, pv)
        ctx[:, cols] = out.astype(jnp.bfloat16)
    attended = jnp.dot(ctx[...], eo_ref[...], preferred_element_type=jnp.float32)
    rows = sp_ref[0].astype(jnp.float32) + attended
    local_row = pl.program_id(1) * QBLOCK + lax.broadcasted_iota(jnp.int32, (QBLOCK, 1), 0)
    encoded = jnp.where(local_row < lim_ref[pl.program_id(0)], rows, 0.0).astype(jnp.bfloat16)
    e_ref[0] = encoded
    pooled_rows = QBLOCK // POOL
    pool_matrix = jnp.where(
        lax.broadcasted_iota(jnp.int32, (pooled_rows, QBLOCK), 1) // POOL
        == lax.broadcasted_iota(jnp.int32, (pooled_rows, QBLOCK), 0),
        1.0 / POOL,
        0.0,
    ).astype(jnp.bfloat16)
    pooled = jnp.dot(pool_matrix, encoded, preferred_element_type=jnp.float32)
    p_ref[0] = pooled.astype(p_ref.dtype)


def band_attention(qkv, keyval_edges, bias_mid, bias_edge, enc_out, spectra, row_limit):
    spec_dev, bin_dev, triple = qkv.shape
    width = triple // 3
    edge_rows = keyval_edges.shape[1] // 2
    groups = width // HGROUP
    qblocks = bin_dev // QBLOCK
    kwin = bin_dev + edge_rows
    pooled_rows = QBLOCK // POOL
    return pl.pallas_call(
        band_kernel,
        out_shape=(
            jax.ShapeDtypeStruct((spec_dev, bin_dev, width), jnp.bfloat16),
            jax.ShapeDtypeStruct((spec_dev, bin_dev // POOL, width), jnp.bfloat16),
        ),
        grid=(spec_dev, qblocks),
        in_specs=[
            pl.BlockSpec((1, QBLOCK, HGROUP), lambda s, b: (s, b, 0)),
            pl.BlockSpec((1, bin_dev, HGROUP), lambda s, b: (s, 0, groups)),
            pl.BlockSpec((1, bin_dev, HGROUP), lambda s, b: (s, 0, 2 * groups)),
            pl.BlockSpec((1, edge_rows, HGROUP), lambda s, b: (s, b, 0)),
            pl.BlockSpec((1, edge_rows, HGROUP), lambda s, b: (s, b, groups)),
            pl.BlockSpec((1, 1, QBLOCK, bin_dev), lambda s, b: (s, b, 0, 0)),
            pl.BlockSpec((1, 1, QBLOCK, edge_rows), lambda s, b: (s, b, 0, 0)),
            pl.BlockSpec((width, width), lambda s, b: (0, 0)),
            pl.BlockSpec((1, QBLOCK, width), lambda s, b: (s, b, 0)),
            pl.BlockSpec(memory_space=pltpu.SMEM),
        ],
        out_specs=(
            pl.BlockSpec((1, QBLOCK, width), lambda s, b: (s, b, 0)),
            pl.BlockSpec((1, pooled_rows, width), lambda s, b: (s, b, 0)),
        ),
        scratch_shapes=[pltpu.VMEM((QBLOCK, width), jnp.bfloat16)],
        compiler_params=pltpu.CompilerParams(dimension_semantics=("arbitrary", "arbitrary")),
        cost_estimate=pl.CostEstimate(
            flops=spec_dev * bin_dev * (kwin * width * 8 + width * width * 2),
            transcendentals=spec_dev * bin_dev * kwin * HE,
            bytes_accessed=spec_dev * bin_dev * width * 14
            + (bias_mid.size + bias_edge.size) * 4
            + width * width * 2,
        ),
    )(
        qkv, qkv, qkv, keyval_edges, keyval_edges, bias_mid, bias_edge,
        enc_out, spectra, row_limit,
    )

def cross_kernel(q_ref, k_ref, v_ref, b_ref, o_ref):
    s = lax.dot_general(
        q_ref[0], k_ref[0], (((1,), (1,)), ((), ())), preferred_element_type=jnp.float32
    )
    s = s * DEC_SCALE + b_ref[0]
    m = jnp.max(s, axis=1, keepdims=True)
    p = jnp.exp(s - m)
    total = jnp.sum(p, axis=1, keepdims=True)
    pv = jnp.dot(p.astype(jnp.bfloat16), v_ref[0], preferred_element_type=jnp.float32)
    o_ref[0] = (pv / total).astype(o_ref.dtype)


def cross_attention(query_one, received, mem_bias, heads_here, dec_head):
    _, all_tok, width = query_one.shape
    mem_len = received.shape[1]
    return pl.pallas_call(
        cross_kernel,
        out_shape=jax.ShapeDtypeStruct(query_one.shape, jnp.bfloat16),
        grid=(heads_here,),
        in_specs=[
            pl.BlockSpec((1, all_tok, dec_head), lambda h: (0, 0, h)),
            pl.BlockSpec((1, mem_len, dec_head), lambda h: (0, 0, h)),
            pl.BlockSpec((1, mem_len, dec_head), lambda h: (0, 0, heads_here + h)),
            pl.BlockSpec((1, 1, mem_len), lambda h: (0, 0, 0)),
        ],
        out_specs=pl.BlockSpec((1, all_tok, dec_head), lambda h: (0, 0, h)),
        cost_estimate=pl.CostEstimate(
            flops=all_tok * mem_len * width * 4,
            transcendentals=all_tok * mem_len * heads_here,
            bytes_accessed=all_tok * width * 4 + mem_len * width * 4,
        ),
    )(query_one, received, received, mem_bias)


def per_device(
    spectra,
    key_bias,
    valid_bins,
    enc_query,
    enc_key,
    enc_value,
    enc_out,
    token_ids,
    embedding,
    dec_query,
    mem_key,
    mem_value,
    dec_out,
):
    seq_pos = lax.axis_index("seq")
    head_pos = lax.axis_index("head")
    spec_dev, bin_dev, model_width = spectra.shape
    half_span = WINDOW // 2
    first_spec = head_pos * spec_dev
    first_bin = seq_pos * bin_dev
    my_counts = lax.dynamic_slice_in_dim(valid_bins, first_spec, spec_dev, 0)
    bias_pad = jnp.pad(key_bias, ((0, 0), (half_span, half_span)))
    my_bias = lax.dynamic_slice(
        bias_pad, (first_spec, first_bin), (spec_dev, bin_dev + 2 * half_span)
    )
    kv_weights = jnp.concatenate([enc_key, enc_value], axis=1)
    qkv_weights = jnp.concatenate([enc_query, enc_key, enc_value], axis=1)

    count = lax.axis_size("seq")
    forward = [(i, i + 1) for i in range(count - 1)]
    backward = [(target, source) for source, target in forward]
    low_edge = lax.ppermute(spectra[:, bin_dev - half_span :], "seq", forward)
    high_edge = lax.ppermute(spectra[:, :half_span], "seq", backward)

    normed = rms_rows(spectra)
    qkv = jnp.einsum(
        "sbd,de->sbe", normed, qkv_weights, preferred_element_type=jnp.float32
    ).astype(jnp.bfloat16)
    edges = rms_rows(jnp.concatenate([low_edge, high_edge], axis=1))
    keyval_edges = jnp.einsum(
        "sbd,de->sbe", edges, kv_weights, preferred_element_type=jnp.float32
    ).astype(jnp.bfloat16)
    key_span = bin_dev + 2 * half_span
    key_cols = first_bin - half_span + jnp.arange(key_span, dtype=jnp.int32)
    col_ok = (key_cols[None, :] >= 0) & (key_cols[None, :] < my_counts[:, None])
    col_bias = jnp.where(col_ok, my_bias, masked_score)
    qblocks = bin_dev // QBLOCK
    block_ix = jnp.arange(qblocks, dtype=jnp.int32)[:, None, None]
    query_local = block_ix * QBLOCK + jnp.arange(QBLOCK, dtype=jnp.int32)[None, :, None]
    key_mid = half_span + jnp.arange(bin_dev, dtype=jnp.int32)[None, None, :]
    key_edge = jnp.arange(half_span, dtype=jnp.int32)[None, None, :] + block_ix * (
        key_span - half_span
    )
    band_mid = (key_mid - query_local >= 0) & (key_mid - query_local <= WINDOW)
    band_edge = (key_edge - query_local >= 0) & (key_edge - query_local <= WINDOW)
    col_mid = col_bias[:, half_span : half_span + bin_dev]
    col_edge = col_bias.reshape(spec_dev, key_span // half_span, half_span)[:, :: qblocks + 1]
    bias_mid = jnp.where(band_mid[None], col_mid[:, None, None, :], masked_score)
    bias_edge = jnp.where(band_edge[None], col_edge[:, :, None, :], masked_score)
    row_limit = my_counts - first_bin
    encoded, pooled = band_attention(
        qkv, keyval_edges, bias_mid, bias_edge, enc_out, spectra, row_limit
    )
    spectra_all = lax.all_gather(pooled, "head", axis=0, tiled=True)
    mem_weights = jnp.concatenate([mem_key, mem_value], axis=1)
    local_width = mem_key.shape[1]
    memory_part = jnp.einsum(
        "spd,de->spe", rms_rows(spectra_all), mem_weights, preferred_element_type=jnp.float32
    ).astype(jnp.bfloat16)
    spec_count, part_len, part_width = memory_part.shape
    tok_count = token_ids.shape[1]
    id_cols = jnp.zeros((spec_count, part_len, 128), jnp.bfloat16)
    id_cols = id_cols.at[:, 0, :tok_count].set(token_ids.astype(jnp.bfloat16))
    payload = jnp.concatenate([memory_part, id_cols], axis=2)
    received = lax.all_to_all(payload, "seq", 0, 1, tiled=True)
    seq_count = lax.axis_size("seq")
    memory = received[:, :, :part_width]
    ids_one = received.reshape(seq_count, part_len, part_width + 128)[:, 0, part_width : part_width + tok_count]
    ids_one = ids_one.reshape(1, seq_count * tok_count).astype(jnp.int32)
    mem_len = memory.shape[1]
    bias_row = lax.dynamic_slice_in_dim(key_bias, seq_pos, 1, 0)
    pooled_bias = jnp.max(bias_row.reshape(1, mem_len, POOL), axis=2)
    count_row = lax.dynamic_slice_in_dim(valid_bins, seq_pos, 1, 0)
    mem_valid = jnp.arange(mem_len, dtype=jnp.int32)[None, :] * POOL < count_row[:, None]
    dec_width = embedding.shape[1]
    dec_head = dec_width // HD
    heads_here = local_width // dec_head
    share_width = dec_width // lax.axis_size("head")
    vocab = embedding.shape[0]
    onehot = (
        token_ids[:, :, None] == jnp.arange(vocab, dtype=jnp.int32)[None, None, :]
    ).astype(jnp.bfloat16)
    own_table = lax.dynamic_slice_in_dim(embedding, head_pos * share_width, share_width, 1)
    own_part = jnp.einsum(
        "stv,vd->std", onehot, own_table, preferred_element_type=jnp.float32
    ).astype(jnp.bfloat16)
    query_table = jnp.einsum(
        "vd,de->ve", rms_rows(embedding), dec_query, preferred_element_type=jnp.float32
    ).astype(jnp.bfloat16)
    query_one = jnp.take(query_table, ids_one[0], axis=0)[None]
    mem_bias = jnp.where(mem_valid, pooled_bias, masked_score)[:, None, :]
    context_one = cross_attention(query_one, received, mem_bias, heads_here, dec_head)
    context_one = context_one.reshape(seq_count, tok_count, local_width)
    dec_context = lax.all_to_all(context_one, "seq", 0, 0, tiled=True)
    partial_sums = jnp.einsum(
        "ste,ed->std", dec_context, dec_out, preferred_element_type=jnp.float32
    )
    summed = lax.psum_scatter(
        partial_sums.astype(jnp.bfloat16), "head", scatter_dimension=2, tiled=True
    ).astype(jnp.float32)
    decoded = (own_part.astype(jnp.float32) + summed).astype(jnp.bfloat16)
    return (encoded, decoded)


def solution(mesh):
    return jax.shard_map(
        per_device,
        mesh=mesh,
        in_specs=(
            P("head", "seq", None),
            P(),
            P(),
            P(),
            P(),
            P(),
            P(),
            P(None, "seq"),
            P(),
            P(None, "head"),
            P(None, "head"),
            P(None, "head"),
            P("head", None),
        ),
        out_specs=(P("head", "seq", None), P(None, "seq", "head")),
        check_vma=False,
    )
```

```python
import jax
import jax.numpy as jnp
from jax import lax
from jax.experimental import pallas as pl
from jax.experimental.pallas import tpu as pltpu
from jax.sharding import PartitionSpec as P

HE = 16
WINDOW = 512
POOL = 32
HD = 32
QBLOCK = 256
HGROUP = 1024
DEC_SCALE = 128 ** (-0.5)


epsilon = 1e-05
masked_score = -1e30


def rms_rows(values_in):
    widened = values_in.astype(jnp.float32)
    inverse_rms = lax.rsqrt(jnp.mean(widened * widened, axis=-1, keepdims=True) + epsilon)
    return (widened * inverse_rms).astype(jnp.bfloat16)


def softmax_rows(scores):
    row_top = jnp.max(scores, axis=-1, keepdims=True)
    weights = jnp.exp(scores - row_top)
    return (weights / jnp.sum(weights, axis=-1, keepdims=True)).astype(jnp.bfloat16)


def band_kernel(
    q_ref, km_ref, vm_ref, ke_ref, ve_ref, bm_ref, be_ref, eo_ref, sp_ref, lim_ref, e_ref, p_ref, ctx
):
    bias_mid = bm_ref[0, 0]
    bias_edge = be_ref[0, 0]
    lane = lax.broadcasted_iota(jnp.int32, (1, 128), 1)
    low = lane < 64
    dims = (((1,), (1,)), ((), ()))
    for pair in range(HGROUP // 128):
        cols = slice(pair * 128, (pair + 1) * 128)
        q = q_ref[0, :, cols] * 0.125
        key_mid = km_ref[0, :, cols]
        key_edge = ke_ref[0, :, cols]
        out = None
        for half in range(2):
            sel = low if half == 0 else jnp.logical_not(low)
            qh = jnp.where(sel, q, jnp.zeros_like(q))
            s_mid = lax.dot_general(qh, key_mid, dims, preferred_element_type=jnp.float32)
            s_mid = s_mid + bias_mid
            s_edge = lax.dot_general(qh, key_edge, dims, preferred_element_type=jnp.float32)
            s_edge = s_edge + bias_edge
            m = jnp.maximum(
                jnp.max(s_mid, axis=1, keepdims=True), jnp.max(s_edge, axis=1, keepdims=True)
            )
            p_mid = jnp.exp(s_mid - m)
            p_edge = jnp.exp(s_edge - m)
            total = jnp.sum(p_mid, axis=1, keepdims=True) + jnp.sum(p_edge, axis=1, keepdims=True)
            pv = jnp.dot(
                p_mid.astype(jnp.bfloat16), vm_ref[0, :, cols], preferred_element_type=jnp.float32
            ) + jnp.dot(
                p_edge.astype(jnp.bfloat16), ve_ref[0, :, cols], preferred_element_type=jnp.float32
            )
            pv = pv / total
            out = pv if out is None else jnp.where(low, out, pv)
        ctx[:, cols] = out.astype(jnp.bfloat16)
    attended = jnp.dot(ctx[...], eo_ref[...], preferred_element_type=jnp.float32)
    rows = sp_ref[0].astype(jnp.float32) + attended
    local_row = pl.program_id(1) * QBLOCK + lax.broadcasted_iota(jnp.int32, (QBLOCK, 1), 0)
    encoded = jnp.where(local_row < lim_ref[pl.program_id(0)], rows, 0.0).astype(jnp.bfloat16)
    e_ref[0] = encoded
    pooled_rows = QBLOCK // POOL
    pool_matrix = jnp.where(
        lax.broadcasted_iota(jnp.int32, (pooled_rows, QBLOCK), 1) // POOL
        == lax.broadcasted_iota(jnp.int32, (pooled_rows, QBLOCK), 0),
        1.0 / POOL,
        0.0,
    ).astype(jnp.bfloat16)
    pooled = jnp.dot(pool_matrix, encoded, preferred_element_type=jnp.float32)
    p_ref[0] = pooled.astype(p_ref.dtype)


def band_attention(qkv, keyval_edges, bias_mid, bias_edge, enc_out, spectra, row_limit):
    spec_dev, bin_dev, triple = qkv.shape
    width = triple // 3
    edge_rows = keyval_edges.shape[1] // 2
    groups = width // HGROUP
    qblocks = bin_dev // QBLOCK
    kwin = bin_dev + edge_rows
    pooled_rows = QBLOCK // POOL
    return pl.pallas_call(
        band_kernel,
        out_shape=(
            jax.ShapeDtypeStruct((spec_dev, bin_dev, width), jnp.bfloat16),
            jax.ShapeDtypeStruct((spec_dev, bin_dev // POOL, width), jnp.bfloat16),
        ),
        grid=(spec_dev, qblocks),
        in_specs=[
            pl.BlockSpec((1, QBLOCK, HGROUP), lambda s, b: (s, b, 0)),
            pl.BlockSpec((1, bin_dev, HGROUP), lambda s, b: (s, 0, groups)),
            pl.BlockSpec((1, bin_dev, HGROUP), lambda s, b: (s, 0, 2 * groups)),
            pl.BlockSpec((1, edge_rows, HGROUP), lambda s, b: (s, b, 0)),
            pl.BlockSpec((1, edge_rows, HGROUP), lambda s, b: (s, b, groups)),
            pl.BlockSpec((1, 1, QBLOCK, bin_dev), lambda s, b: (s, b, 0, 0)),
            pl.BlockSpec((1, 1, QBLOCK, edge_rows), lambda s, b: (s, b, 0, 0)),
            pl.BlockSpec((width, width), lambda s, b: (0, 0)),
            pl.BlockSpec((1, QBLOCK, width), lambda s, b: (s, b, 0)),
            pl.BlockSpec(memory_space=pltpu.SMEM),
        ],
        out_specs=(
            pl.BlockSpec((1, QBLOCK, width), lambda s, b: (s, b, 0)),
            pl.BlockSpec((1, pooled_rows, width), lambda s, b: (s, b, 0)),
        ),
        scratch_shapes=[pltpu.VMEM((QBLOCK, width), jnp.bfloat16)],
        compiler_params=pltpu.CompilerParams(dimension_semantics=("arbitrary", "arbitrary")),
        cost_estimate=pl.CostEstimate(
            flops=spec_dev * bin_dev * (kwin * width * 8 + width * width * 2),
            transcendentals=spec_dev * bin_dev * kwin * HE,
            bytes_accessed=spec_dev * bin_dev * width * 14
            + (bias_mid.size + bias_edge.size) * 4
            + width * width * 2,
        ),
    )(
        qkv, qkv, qkv, keyval_edges, keyval_edges, bias_mid, bias_edge,
        enc_out, spectra, row_limit,
    )

def cross_kernel(q_ref, k_ref, v_ref, b_ref, o_ref):
    s = lax.dot_general(
        q_ref[0], k_ref[0], (((1,), (1,)), ((), ())), preferred_element_type=jnp.float32
    )
    s = s * DEC_SCALE + b_ref[0]
    m = jnp.max(s, axis=1, keepdims=True)
    p = jnp.exp(s - m)
    total = jnp.sum(p, axis=1, keepdims=True)
    pv = jnp.dot(p.astype(jnp.bfloat16), v_ref[0], preferred_element_type=jnp.float32)
    o_ref[0] = (pv / total).astype(o_ref.dtype)


def cross_attention(query_one, received, mem_bias, heads_here, dec_head):
    _, all_tok, width = query_one.shape
    mem_len = received.shape[1]
    return pl.pallas_call(
        cross_kernel,
        out_shape=jax.ShapeDtypeStruct(query_one.shape, jnp.bfloat16),
        grid=(heads_here,),
        in_specs=[
            pl.BlockSpec((1, all_tok, dec_head), lambda h: (0, 0, h)),
            pl.BlockSpec((1, mem_len, dec_head), lambda h: (0, 0, h)),
            pl.BlockSpec((1, mem_len, dec_head), lambda h: (0, 0, heads_here + h)),
            pl.BlockSpec((1, 1, mem_len), lambda h: (0, 0, 0)),
        ],
        out_specs=pl.BlockSpec((1, all_tok, dec_head), lambda h: (0, 0, h)),
        cost_estimate=pl.CostEstimate(
            flops=all_tok * mem_len * width * 4,
            transcendentals=all_tok * mem_len * heads_here,
            bytes_accessed=all_tok * width * 4 + mem_len * width * 4,
        ),
    )(query_one, received, received, mem_bias)


def per_device(
    spectra,
    key_bias,
    valid_bins,
    enc_query,
    enc_key,
    enc_value,
    enc_out,
    token_ids,
    embedding,
    dec_query,
    mem_key,
    mem_value,
    dec_out,
):
    seq_pos = lax.axis_index("seq")
    head_pos = lax.axis_index("head")
    spec_dev, bin_dev, model_width = spectra.shape
    half_span = WINDOW // 2
    first_spec = head_pos * spec_dev
    first_bin = seq_pos * bin_dev
    my_counts = lax.dynamic_slice_in_dim(valid_bins, first_spec, spec_dev, 0)
    bias_pad = jnp.pad(key_bias, ((0, 0), (half_span, half_span)))
    my_bias = lax.dynamic_slice(
        bias_pad, (first_spec, first_bin), (spec_dev, bin_dev + 2 * half_span)
    )
    kv_weights = jnp.concatenate([enc_key, enc_value], axis=1)
    qkv_weights = jnp.concatenate([enc_query, enc_key, enc_value], axis=1)

    count = lax.axis_size("seq")
    forward = [(i, i + 1) for i in range(count - 1)]
    backward = [(target, source) for source, target in forward]
    low_edge = lax.ppermute(spectra[:, bin_dev - half_span :], "seq", forward)
    high_edge = lax.ppermute(spectra[:, :half_span], "seq", backward)

    normed = rms_rows(spectra)
    qkv = jnp.einsum(
        "sbd,de->sbe", normed, qkv_weights, preferred_element_type=jnp.float32
    ).astype(jnp.bfloat16)
    query_table = jnp.einsum(
        "vd,de->ve", rms_rows(embedding), dec_query, preferred_element_type=jnp.float32
    ).astype(jnp.bfloat16)
    query_table, low_edge, high_edge = lax.optimization_barrier(
        (query_table, low_edge, high_edge)
    )
    edges = rms_rows(jnp.concatenate([low_edge, high_edge], axis=1))
    keyval_edges = jnp.einsum(
        "sbd,de->sbe", edges, kv_weights, preferred_element_type=jnp.float32
    ).astype(jnp.bfloat16)
    key_span = bin_dev + 2 * half_span
    key_cols = first_bin - half_span + jnp.arange(key_span, dtype=jnp.int32)
    col_ok = (key_cols[None, :] >= 0) & (key_cols[None, :] < my_counts[:, None])
    col_bias = jnp.where(col_ok, my_bias, masked_score)
    qblocks = bin_dev // QBLOCK
    block_ix = jnp.arange(qblocks, dtype=jnp.int32)[:, None, None]
    query_local = block_ix * QBLOCK + jnp.arange(QBLOCK, dtype=jnp.int32)[None, :, None]
    key_mid = half_span + jnp.arange(bin_dev, dtype=jnp.int32)[None, None, :]
    key_edge = jnp.arange(half_span, dtype=jnp.int32)[None, None, :] + block_ix * (
        key_span - half_span
    )
    band_mid = (key_mid - query_local >= 0) & (key_mid - query_local <= WINDOW)
    band_edge = (key_edge - query_local >= 0) & (key_edge - query_local <= WINDOW)
    col_mid = col_bias[:, half_span : half_span + bin_dev]
    col_edge = col_bias.reshape(spec_dev, key_span // half_span, half_span)[:, :: qblocks + 1]
    bias_mid = jnp.where(band_mid[None], col_mid[:, None, None, :], masked_score)
    bias_edge = jnp.where(band_edge[None], col_edge[:, :, None, :], masked_score)
    row_limit = my_counts - first_bin
    encoded, pooled = band_attention(
        qkv, keyval_edges, bias_mid, bias_edge, enc_out, spectra, row_limit
    )
    spectra_all = lax.all_gather(pooled, "head", axis=0, tiled=True)
    mem_weights = jnp.concatenate([mem_key, mem_value], axis=1)
    local_width = mem_key.shape[1]
    memory_part = jnp.einsum(
        "spd,de->spe", rms_rows(spectra_all), mem_weights, preferred_element_type=jnp.float32
    ).astype(jnp.bfloat16)
    spec_count, part_len, part_width = memory_part.shape
    tok_count = token_ids.shape[1]
    id_cols = jnp.zeros((spec_count, part_len, 128), jnp.bfloat16)
    id_cols = id_cols.at[:, 0, :tok_count].set(token_ids.astype(jnp.bfloat16))
    payload = jnp.concatenate([memory_part, id_cols], axis=2)
    received = lax.all_to_all(payload, "seq", 0, 1, tiled=True)
    seq_count = lax.axis_size("seq")
    memory = received[:, :, :part_width]
    ids_one = received.reshape(seq_count, part_len, part_width + 128)[:, 0, part_width : part_width + tok_count]
    ids_one = ids_one.reshape(1, seq_count * tok_count).astype(jnp.int32)
    mem_len = memory.shape[1]
    bias_row = lax.dynamic_slice_in_dim(key_bias, seq_pos, 1, 0)
    pooled_bias = jnp.max(bias_row.reshape(1, mem_len, POOL), axis=2)
    count_row = lax.dynamic_slice_in_dim(valid_bins, seq_pos, 1, 0)
    mem_valid = jnp.arange(mem_len, dtype=jnp.int32)[None, :] * POOL < count_row[:, None]
    dec_width = embedding.shape[1]
    dec_head = dec_width // HD
    heads_here = local_width // dec_head
    share_width = dec_width // lax.axis_size("head")
    vocab = embedding.shape[0]
    onehot = (
        token_ids[:, :, None] == jnp.arange(vocab, dtype=jnp.int32)[None, None, :]
    ).astype(jnp.bfloat16)
    own_table = lax.dynamic_slice_in_dim(embedding, head_pos * share_width, share_width, 1)
    own_part = jnp.einsum(
        "stv,vd->std", onehot, own_table, preferred_element_type=jnp.float32
    ).astype(jnp.bfloat16)
    query_one = jnp.take(query_table, ids_one[0], axis=0)[None]
    mem_bias = jnp.where(mem_valid, pooled_bias, masked_score)[:, None, :]
    context_one = cross_attention(query_one, received, mem_bias, heads_here, dec_head)
    context_one = context_one.reshape(seq_count, tok_count, local_width)
    dec_context = lax.all_to_all(context_one, "seq", 0, 0, tiled=True)
    partial_sums = jnp.einsum(
        "ste,ed->std", dec_context, dec_out, preferred_element_type=jnp.float32
    )
    summed = lax.psum_scatter(
        partial_sums.astype(jnp.bfloat16), "head", scatter_dimension=2, tiled=True
    ).astype(jnp.float32)
    decoded = (own_part.astype(jnp.float32) + summed).astype(jnp.bfloat16)
    return (encoded, decoded)


def solution(mesh):
    return jax.shard_map(
        per_device,
        mesh=mesh,
        in_specs=(
            P("head", "seq", None),
            P(),
            P(),
            P(),
            P(),
            P(),
            P(),
            P(None, "seq"),
            P(),
            P(None, "head"),
            P(None, "head"),
            P(None, "head"),
            P("head", None),
        ),
        out_specs=(P("head", "seq", None), P(None, "seq", "head")),
        check_vma=False,
    )
```

```python
import jax
import jax.numpy as jnp
from jax import lax
from jax.experimental import pallas as pl
from jax.experimental.pallas import tpu as pltpu
from jax.sharding import PartitionSpec as P

HE = 16
WINDOW = 512
POOL = 32
HD = 32
QBLOCK = 256
HGROUP = 1024
DEC_SCALE = 128 ** (-0.5)


epsilon = 1e-05
masked_score = -1e30


def rms_rows(values_in):
    widened = values_in.astype(jnp.float32)
    inverse_rms = lax.rsqrt(jnp.mean(widened * widened, axis=-1, keepdims=True) + epsilon)
    return (widened * inverse_rms).astype(jnp.bfloat16)


def softmax_rows(scores):
    row_top = jnp.max(scores, axis=-1, keepdims=True)
    weights = jnp.exp(scores - row_top)
    return (weights / jnp.sum(weights, axis=-1, keepdims=True)).astype(jnp.bfloat16)


def band_kernel(
    q_ref, km_ref, vm_ref, ke_ref, ve_ref, bm_ref, be_ref, eo_ref, sp_ref, lim_ref, e_ref, p_ref, ctx
):
    bias_mid = bm_ref[0, 0]
    bias_edge = be_ref[0, 0]
    lane = lax.broadcasted_iota(jnp.int32, (1, 128), 1)
    low = lane < 64
    dims = (((1,), (1,)), ((), ()))
    for pair in range(HGROUP // 128):
        cols = slice(pair * 128, (pair + 1) * 128)
        q = q_ref[0, :, cols] * 0.125
        key_mid = km_ref[0, :, cols]
        key_edge = ke_ref[0, :, cols]
        out = None
        for half in range(2):
            sel = low if half == 0 else jnp.logical_not(low)
            qh = jnp.where(sel, q, jnp.zeros_like(q))
            s_mid = lax.dot_general(qh, key_mid, dims, preferred_element_type=jnp.float32)
            s_mid = s_mid + bias_mid
            s_edge = lax.dot_general(qh, key_edge, dims, preferred_element_type=jnp.float32)
            s_edge = s_edge + bias_edge
            m = jnp.maximum(
                jnp.max(s_mid, axis=1, keepdims=True), jnp.max(s_edge, axis=1, keepdims=True)
            )
            p_mid = jnp.exp(s_mid - m)
            p_edge = jnp.exp(s_edge - m)
            total = jnp.sum(p_mid, axis=1, keepdims=True) + jnp.sum(p_edge, axis=1, keepdims=True)
            pv = jnp.dot(
                p_mid.astype(jnp.bfloat16), vm_ref[0, :, cols], preferred_element_type=jnp.float32
            ) + jnp.dot(
                p_edge.astype(jnp.bfloat16), ve_ref[0, :, cols], preferred_element_type=jnp.float32
            )
            pv = pv / total
            out = pv if out is None else jnp.where(low, out, pv)
        ctx[:, cols] = out.astype(jnp.bfloat16)
    attended = jnp.dot(ctx[...], eo_ref[...], preferred_element_type=jnp.float32)
    rows = sp_ref[0].astype(jnp.float32) + attended
    local_row = pl.program_id(1) * QBLOCK + lax.broadcasted_iota(jnp.int32, (QBLOCK, 1), 0)
    encoded = jnp.where(local_row < lim_ref[pl.program_id(0)], rows, 0.0).astype(jnp.bfloat16)
    e_ref[0] = encoded
    pooled_rows = QBLOCK // POOL
    pool_matrix = jnp.where(
        lax.broadcasted_iota(jnp.int32, (pooled_rows, QBLOCK), 1) // POOL
        == lax.broadcasted_iota(jnp.int32, (pooled_rows, QBLOCK), 0),
        1.0 / POOL,
        0.0,
    ).astype(jnp.bfloat16)
    pooled = jnp.dot(pool_matrix, encoded, preferred_element_type=jnp.float32)
    p_ref[0] = pooled.astype(p_ref.dtype)


def band_attention(qkv, keyval_edges, bias_mid, bias_edge, enc_out, spectra, row_limit):
    spec_dev, bin_dev, triple = qkv.shape
    width = triple // 3
    edge_rows = keyval_edges.shape[1] // 2
    groups = width // HGROUP
    qblocks = bin_dev // QBLOCK
    kwin = bin_dev + edge_rows
    pooled_rows = QBLOCK // POOL
    return pl.pallas_call(
        band_kernel,
        out_shape=(
            jax.ShapeDtypeStruct((spec_dev, bin_dev, width), jnp.bfloat16),
            jax.ShapeDtypeStruct((spec_dev, bin_dev // POOL, width), jnp.bfloat16),
        ),
        grid=(spec_dev, qblocks),
        in_specs=[
            pl.BlockSpec((1, QBLOCK, HGROUP), lambda s, b: (s, b, 0)),
            pl.BlockSpec((1, bin_dev, HGROUP), lambda s, b: (s, 0, groups)),
            pl.BlockSpec((1, bin_dev, HGROUP), lambda s, b: (s, 0, 2 * groups)),
            pl.BlockSpec((1, edge_rows, HGROUP), lambda s, b: (s, b, 0)),
            pl.BlockSpec((1, edge_rows, HGROUP), lambda s, b: (s, b, groups)),
            pl.BlockSpec((1, 1, QBLOCK, bin_dev), lambda s, b: (s, b, 0, 0)),
            pl.BlockSpec((1, 1, QBLOCK, edge_rows), lambda s, b: (s, b, 0, 0)),
            pl.BlockSpec((width, width), lambda s, b: (0, 0)),
            pl.BlockSpec((1, QBLOCK, width), lambda s, b: (s, b, 0)),
            pl.BlockSpec(memory_space=pltpu.SMEM),
        ],
        out_specs=(
            pl.BlockSpec((1, QBLOCK, width), lambda s, b: (s, b, 0)),
            pl.BlockSpec((1, pooled_rows, width), lambda s, b: (s, b, 0)),
        ),
        scratch_shapes=[pltpu.VMEM((QBLOCK, width), jnp.bfloat16)],
        compiler_params=pltpu.CompilerParams(dimension_semantics=("arbitrary", "arbitrary")),
        cost_estimate=pl.CostEstimate(
            flops=spec_dev * bin_dev * (kwin * width * 8 + width * width * 2),
            transcendentals=spec_dev * bin_dev * kwin * HE,
            bytes_accessed=spec_dev * bin_dev * width * 14
            + (bias_mid.size + bias_edge.size) * 4
            + width * width * 2,
        ),
    )(
        qkv, qkv, qkv, keyval_edges, keyval_edges, bias_mid, bias_edge,
        enc_out, spectra, row_limit,
    )

def cross_kernel(q_ref, k_ref, v_ref, b_ref, o_ref):
    s = lax.dot_general(
        q_ref[0], k_ref[0], (((1,), (1,)), ((), ())), preferred_element_type=jnp.float32
    )
    s = s * DEC_SCALE + b_ref[0]
    m = jnp.max(s, axis=1, keepdims=True)
    p = jnp.exp(s - m)
    total = jnp.sum(p, axis=1, keepdims=True)
    pv = jnp.dot(p.astype(jnp.bfloat16), v_ref[0], preferred_element_type=jnp.float32)
    o_ref[0] = (pv / total).astype(o_ref.dtype)


def cross_attention(query_one, received, mem_bias, heads_here, dec_head):
    _, all_tok, width = query_one.shape
    mem_len = received.shape[1]
    return pl.pallas_call(
        cross_kernel,
        out_shape=jax.ShapeDtypeStruct(query_one.shape, jnp.bfloat16),
        grid=(heads_here,),
        in_specs=[
            pl.BlockSpec((1, all_tok, dec_head), lambda h: (0, 0, h)),
            pl.BlockSpec((1, mem_len, dec_head), lambda h: (0, 0, h)),
            pl.BlockSpec((1, mem_len, dec_head), lambda h: (0, 0, heads_here + h)),
            pl.BlockSpec((1, 1, mem_len), lambda h: (0, 0, 0)),
        ],
        out_specs=pl.BlockSpec((1, all_tok, dec_head), lambda h: (0, 0, h)),
        cost_estimate=pl.CostEstimate(
            flops=all_tok * mem_len * width * 4,
            transcendentals=all_tok * mem_len * heads_here,
            bytes_accessed=all_tok * width * 4 + mem_len * width * 4,
        ),
    )(query_one, received, received, mem_bias)


def per_device(
    spectra,
    key_bias,
    valid_bins,
    enc_query,
    enc_key,
    enc_value,
    enc_out,
    token_ids,
    embedding,
    dec_query,
    mem_key,
    mem_value,
    dec_out,
):
    seq_pos = lax.axis_index("seq")
    head_pos = lax.axis_index("head")
    spec_dev, bin_dev, model_width = spectra.shape
    half_span = WINDOW // 2
    first_spec = head_pos * spec_dev
    first_bin = seq_pos * bin_dev
    my_counts = lax.dynamic_slice_in_dim(valid_bins, first_spec, spec_dev, 0)
    bias_pad = jnp.pad(key_bias, ((0, 0), (half_span, half_span)))
    my_bias = lax.dynamic_slice(
        bias_pad, (first_spec, first_bin), (spec_dev, bin_dev + 2 * half_span)
    )
    kv_weights = jnp.concatenate([enc_key, enc_value], axis=1)
    qkv_weights = jnp.concatenate([enc_query, enc_key, enc_value], axis=1)

    count = lax.axis_size("seq")
    forward = [(i, i + 1) for i in range(count - 1)]
    backward = [(target, source) for source, target in forward]
    low_edge = lax.ppermute(spectra[:, bin_dev - half_span :], "seq", forward)
    high_edge = lax.ppermute(spectra[:, :half_span], "seq", backward)

    normed = rms_rows(spectra)
    qkv = jnp.einsum(
        "sbd,de->sbe", normed, qkv_weights, preferred_element_type=jnp.float32
    ).astype(jnp.bfloat16)
    query_table = jnp.einsum(
        "vd,de->ve", rms_rows(embedding), dec_query, preferred_element_type=jnp.float32
    ).astype(jnp.bfloat16)
    query_table, low_edge, high_edge = lax.optimization_barrier(
        (query_table, low_edge, high_edge)
    )
    edges = rms_rows(jnp.concatenate([low_edge, high_edge], axis=1))
    keyval_edges = jnp.einsum(
        "sbd,de->sbe", edges, kv_weights, preferred_element_type=jnp.float32
    ).astype(jnp.bfloat16)
    key_span = bin_dev + 2 * half_span
    key_cols = first_bin - half_span + jnp.arange(key_span, dtype=jnp.int32)
    col_ok = (key_cols[None, :] >= 0) & (key_cols[None, :] < my_counts[:, None])
    col_bias = jnp.where(col_ok, my_bias, masked_score)
    qblocks = bin_dev // QBLOCK
    block_ix = jnp.arange(qblocks, dtype=jnp.int32)[:, None, None]
    query_local = block_ix * QBLOCK + jnp.arange(QBLOCK, dtype=jnp.int32)[None, :, None]
    key_mid = half_span + jnp.arange(bin_dev, dtype=jnp.int32)[None, None, :]
    key_edge = jnp.arange(half_span, dtype=jnp.int32)[None, None, :] + block_ix * (
        key_span - half_span
    )
    band_mid = (key_mid - query_local >= 0) & (key_mid - query_local <= WINDOW)
    band_edge = (key_edge - query_local >= 0) & (key_edge - query_local <= WINDOW)
    col_mid = col_bias[:, half_span : half_span + bin_dev]
    col_edge = col_bias.reshape(spec_dev, key_span // half_span, half_span)[:, :: qblocks + 1]
    bias_mid = jnp.where(band_mid[None], col_mid[:, None, None, :], masked_score)
    bias_edge = jnp.where(band_edge[None], col_edge[:, :, None, :], masked_score)
    row_limit = my_counts - first_bin
    encoded, pooled = band_attention(
        qkv, keyval_edges, bias_mid, bias_edge, enc_out, spectra, row_limit
    )
    spectra_all = lax.all_gather(pooled, "head", axis=0, tiled=True)
    mem_weights = jnp.concatenate([mem_key, mem_value], axis=1)
    local_width = mem_key.shape[1]
    memory_part = jnp.einsum(
        "spd,de->spe", rms_rows(spectra_all), mem_weights, preferred_element_type=jnp.float32
    ).astype(jnp.bfloat16)
    spec_count, part_len, part_width = memory_part.shape
    tok_count = token_ids.shape[1]
    id_cols = jnp.zeros((spec_count, part_len, 128), jnp.bfloat16)
    id_cols = id_cols.at[:, 0, :tok_count].set(token_ids.astype(jnp.bfloat16))
    payload = jnp.concatenate([memory_part, id_cols], axis=2)
    received = lax.all_to_all(payload, "seq", 0, 1, tiled=True)
    seq_count = lax.axis_size("seq")
    memory = received[:, :, :part_width]
    ids_one = received.reshape(seq_count, part_len, part_width + 128)[:, 0, part_width : part_width + tok_count]
    ids_one = ids_one.reshape(1, seq_count * tok_count).astype(jnp.int32)
    mem_len = memory.shape[1]
    bias_row = lax.dynamic_slice_in_dim(key_bias, seq_pos, 1, 0)
    pooled_bias = jnp.max(bias_row.reshape(1, mem_len, POOL), axis=2)
    count_row = lax.dynamic_slice_in_dim(valid_bins, seq_pos, 1, 0)
    mem_valid = jnp.arange(mem_len, dtype=jnp.int32)[None, :] * POOL < count_row[:, None]
    dec_width = embedding.shape[1]
    dec_head = dec_width // HD
    heads_here = local_width // dec_head
    share_width = dec_width // lax.axis_size("head")
    vocab = embedding.shape[0]
    own_table = lax.dynamic_slice_in_dim(embedding, head_pos * share_width, share_width, 1)
    own_part = jnp.take(own_table, token_ids, axis=0)
    own_part, received = lax.optimization_barrier((own_part, received))
    query_one = jnp.take(query_table, ids_one[0], axis=0)[None]
    mem_bias = jnp.where(mem_valid, pooled_bias, masked_score)[:, None, :]
    context_one = cross_attention(query_one, received, mem_bias, heads_here, dec_head)
    context_one = context_one.reshape(seq_count, tok_count, local_width)
    dec_context = lax.all_to_all(context_one, "seq", 0, 0, tiled=True)
    partial_sums = jnp.einsum(
        "ste,ed->std", dec_context, dec_out, preferred_element_type=jnp.float32
    )
    summed = lax.psum_scatter(
        partial_sums.astype(jnp.bfloat16), "head", scatter_dimension=2, tiled=True
    ).astype(jnp.float32)
    decoded = (own_part.astype(jnp.float32) + summed).astype(jnp.bfloat16)
    return (encoded, decoded)


def solution(mesh):
    return jax.shard_map(
        per_device,
        mesh=mesh,
        in_specs=(
            P("head", "seq", None),
            P(),
            P(),
            P(),
            P(),
            P(),
            P(),
            P(None, "seq"),
            P(),
            P(None, "head"),
            P(None, "head"),
            P(None, "head"),
            P("head", None),
        ),
        out_specs=(P("head", "seq", None), P(None, "seq", "head")),
        check_vma=False,
    )
```

```python
import jax
import jax.numpy as jnp
from jax import lax
from jax.experimental import pallas as pl
from jax.experimental.pallas import tpu as pltpu
from jax.sharding import PartitionSpec as P

HE = 16
WINDOW = 512
POOL = 32
HD = 32
QBLOCK = 256
HGROUP = 1024
DEC_SCALE = 128 ** (-0.5)


epsilon = 1e-05
masked_score = -1e30


def rms_rows(values_in):
    widened = values_in.astype(jnp.float32)
    inverse_rms = lax.rsqrt(jnp.mean(widened * widened, axis=-1, keepdims=True) + epsilon)
    return (widened * inverse_rms).astype(jnp.bfloat16)


def softmax_rows(scores):
    row_top = jnp.max(scores, axis=-1, keepdims=True)
    weights = jnp.exp(scores - row_top)
    return (weights / jnp.sum(weights, axis=-1, keepdims=True)).astype(jnp.bfloat16)


def band_kernel(
    q_ref, km_ref, vm_ref, ke_ref, ve_ref, bm_ref, be_ref, eo_ref, sp_ref, lim_ref, e_ref, p_ref, ctx
):
    bias_mid = bm_ref[0, 0]
    bias_edge = be_ref[0, 0]
    lane = lax.broadcasted_iota(jnp.int32, (1, 128), 1)
    low = lane < 64
    dims = (((1,), (1,)), ((), ()))
    for pair in range(HGROUP // 128):
        cols = slice(pair * 128, (pair + 1) * 128)
        q = q_ref[0, :, cols] * 0.125
        key_mid = km_ref[0, :, cols]
        key_edge = ke_ref[0, :, cols]
        out = None
        for half in range(2):
            sel = low if half == 0 else jnp.logical_not(low)
            qh = jnp.where(sel, q, jnp.zeros_like(q))
            s_mid = lax.dot_general(qh, key_mid, dims, preferred_element_type=jnp.float32)
            s_mid = s_mid + bias_mid
            s_edge = lax.dot_general(qh, key_edge, dims, preferred_element_type=jnp.float32)
            s_edge = s_edge + bias_edge
            m = jnp.maximum(
                jnp.max(s_mid, axis=1, keepdims=True), jnp.max(s_edge, axis=1, keepdims=True)
            )
            p_mid = jnp.exp(s_mid - m)
            p_edge = jnp.exp(s_edge - m)
            total = jnp.sum(p_mid, axis=1, keepdims=True) + jnp.sum(p_edge, axis=1, keepdims=True)
            pv = jnp.dot(
                p_mid.astype(jnp.bfloat16), vm_ref[0, :, cols], preferred_element_type=jnp.float32
            ) + jnp.dot(
                p_edge.astype(jnp.bfloat16), ve_ref[0, :, cols], preferred_element_type=jnp.float32
            )
            pv = pv / total
            out = pv if out is None else jnp.where(low, out, pv)
        ctx[:, cols] = out.astype(jnp.bfloat16)
    attended = jnp.dot(ctx[...], eo_ref[...], preferred_element_type=jnp.float32)
    rows = sp_ref[0].astype(jnp.float32) + attended
    local_row = pl.program_id(1) * QBLOCK + lax.broadcasted_iota(jnp.int32, (QBLOCK, 1), 0)
    encoded = jnp.where(local_row < lim_ref[pl.program_id(0)], rows, 0.0).astype(jnp.bfloat16)
    e_ref[0] = encoded
    pooled_rows = QBLOCK // POOL
    pool_matrix = jnp.where(
        lax.broadcasted_iota(jnp.int32, (pooled_rows, QBLOCK), 1) // POOL
        == lax.broadcasted_iota(jnp.int32, (pooled_rows, QBLOCK), 0),
        1.0 / POOL,
        0.0,
    ).astype(jnp.bfloat16)
    pooled = jnp.dot(pool_matrix, encoded, preferred_element_type=jnp.float32)
    p_ref[0] = pooled.astype(p_ref.dtype)


def band_attention(qkv, keyval_edges, bias_mid, bias_edge, enc_out, spectra, row_limit):
    spec_dev, bin_dev, triple = qkv.shape
    width = triple // 3
    edge_rows = keyval_edges.shape[1] // 2
    groups = width // HGROUP
    qblocks = bin_dev // QBLOCK
    kwin = bin_dev + edge_rows
    pooled_rows = QBLOCK // POOL
    return pl.pallas_call(
        band_kernel,
        out_shape=(
            jax.ShapeDtypeStruct((spec_dev, bin_dev, width), jnp.bfloat16),
            jax.ShapeDtypeStruct((spec_dev, bin_dev // POOL, width), jnp.bfloat16),
        ),
        grid=(spec_dev, qblocks),
        in_specs=[
            pl.BlockSpec((1, QBLOCK, HGROUP), lambda s, b: (s, b, 0)),
            pl.BlockSpec((1, bin_dev, HGROUP), lambda s, b: (s, 0, groups)),
            pl.BlockSpec((1, bin_dev, HGROUP), lambda s, b: (s, 0, 2 * groups)),
            pl.BlockSpec((1, edge_rows, HGROUP), lambda s, b: (s, b, 0)),
            pl.BlockSpec((1, edge_rows, HGROUP), lambda s, b: (s, b, groups)),
            pl.BlockSpec((1, 1, QBLOCK, bin_dev), lambda s, b: (s, b, 0, 0)),
            pl.BlockSpec((1, 1, QBLOCK, edge_rows), lambda s, b: (s, b, 0, 0)),
            pl.BlockSpec((width, width), lambda s, b: (0, 0)),
            pl.BlockSpec((1, QBLOCK, width), lambda s, b: (s, b, 0)),
            pl.BlockSpec(memory_space=pltpu.SMEM),
        ],
        out_specs=(
            pl.BlockSpec((1, QBLOCK, width), lambda s, b: (s, b, 0)),
            pl.BlockSpec((1, pooled_rows, width), lambda s, b: (s, b, 0)),
        ),
        scratch_shapes=[pltpu.VMEM((QBLOCK, width), jnp.bfloat16)],
        compiler_params=pltpu.CompilerParams(dimension_semantics=("arbitrary", "arbitrary")),
        cost_estimate=pl.CostEstimate(
            flops=spec_dev * bin_dev * (kwin * width * 8 + width * width * 2),
            transcendentals=spec_dev * bin_dev * kwin * HE,
            bytes_accessed=spec_dev * bin_dev * width * 14
            + (bias_mid.size + bias_edge.size) * 4
            + width * width * 2,
        ),
    )(
        qkv, qkv, qkv, keyval_edges, keyval_edges, bias_mid, bias_edge,
        enc_out, spectra, row_limit,
    )

def cross_kernel(q_ref, k_ref, v_ref, b_ref, o_ref):
    s = lax.dot_general(
        q_ref[0], k_ref[0], (((1,), (1,)), ((), ())), preferred_element_type=jnp.float32
    )
    s = s * DEC_SCALE + b_ref[0]
    m = jnp.max(s, axis=1, keepdims=True)
    p = jnp.exp(s - m)
    total = jnp.sum(p, axis=1, keepdims=True)
    pv = jnp.dot(p.astype(jnp.bfloat16), v_ref[0], preferred_element_type=jnp.float32)
    o_ref[0] = (pv / total).astype(o_ref.dtype)


def cross_attention(query_one, received, mem_bias, heads_here, dec_head):
    _, all_tok, width = query_one.shape
    mem_len = received.shape[1]
    return pl.pallas_call(
        cross_kernel,
        out_shape=jax.ShapeDtypeStruct(query_one.shape, jnp.bfloat16),
        grid=(heads_here,),
        in_specs=[
            pl.BlockSpec((1, all_tok, dec_head), lambda h: (0, 0, h)),
            pl.BlockSpec((1, mem_len, dec_head), lambda h: (0, 0, h)),
            pl.BlockSpec((1, mem_len, dec_head), lambda h: (0, 0, heads_here + h)),
            pl.BlockSpec((1, 1, mem_len), lambda h: (0, 0, 0)),
        ],
        out_specs=pl.BlockSpec((1, all_tok, dec_head), lambda h: (0, 0, h)),
        cost_estimate=pl.CostEstimate(
            flops=all_tok * mem_len * width * 4,
            transcendentals=all_tok * mem_len * heads_here,
            bytes_accessed=all_tok * width * 4 + mem_len * width * 4,
        ),
    )(query_one, received, received, mem_bias)


def per_device(
    spectra,
    key_bias,
    valid_bins,
    enc_query,
    enc_key,
    enc_value,
    enc_out,
    token_ids,
    embedding,
    dec_query,
    mem_key,
    mem_value,
    dec_out,
):
    seq_pos = lax.axis_index("seq")
    head_pos = lax.axis_index("head")
    spec_dev, bin_dev, model_width = spectra.shape
    half_span = WINDOW // 2
    first_spec = head_pos * spec_dev
    first_bin = seq_pos * bin_dev
    my_counts = lax.dynamic_slice_in_dim(valid_bins, first_spec, spec_dev, 0)
    bias_pad = jnp.pad(key_bias, ((0, 0), (half_span, half_span)))
    my_bias = lax.dynamic_slice(
        bias_pad, (first_spec, first_bin), (spec_dev, bin_dev + 2 * half_span)
    )
    kv_weights = jnp.concatenate([enc_key, enc_value], axis=1)
    qkv_weights = jnp.concatenate([enc_query, enc_key, enc_value], axis=1)

    count = lax.axis_size("seq")
    forward = [(i, i + 1) for i in range(count - 1)]
    backward = [(target, source) for source, target in forward]
    low_edge = lax.ppermute(spectra[:, bin_dev - half_span :], "seq", forward)
    high_edge = lax.ppermute(spectra[:, :half_span], "seq", backward)

    normed = rms_rows(spectra)
    qkv = jnp.einsum(
        "sbd,de->sbe", normed, qkv_weights, preferred_element_type=jnp.float32
    ).astype(jnp.bfloat16)
    query_table = jnp.einsum(
        "vd,de->ve", rms_rows(embedding), dec_query, preferred_element_type=jnp.float32
    ).astype(jnp.bfloat16)
    mem_weights = jnp.concatenate([mem_key, mem_value], axis=1)
    query_table, mem_weights, low_edge, high_edge = lax.optimization_barrier(
        (query_table, mem_weights, low_edge, high_edge)
    )
    edges = rms_rows(jnp.concatenate([low_edge, high_edge], axis=1))
    keyval_edges = jnp.einsum(
        "sbd,de->sbe", edges, kv_weights, preferred_element_type=jnp.float32
    ).astype(jnp.bfloat16)
    key_span = bin_dev + 2 * half_span
    key_cols = first_bin - half_span + jnp.arange(key_span, dtype=jnp.int32)
    col_ok = (key_cols[None, :] >= 0) & (key_cols[None, :] < my_counts[:, None])
    col_bias = jnp.where(col_ok, my_bias, masked_score)
    qblocks = bin_dev // QBLOCK
    block_ix = jnp.arange(qblocks, dtype=jnp.int32)[:, None, None]
    query_local = block_ix * QBLOCK + jnp.arange(QBLOCK, dtype=jnp.int32)[None, :, None]
    key_mid = half_span + jnp.arange(bin_dev, dtype=jnp.int32)[None, None, :]
    key_edge = jnp.arange(half_span, dtype=jnp.int32)[None, None, :] + block_ix * (
        key_span - half_span
    )
    band_mid = (key_mid - query_local >= 0) & (key_mid - query_local <= WINDOW)
    band_edge = (key_edge - query_local >= 0) & (key_edge - query_local <= WINDOW)
    col_mid = col_bias[:, half_span : half_span + bin_dev]
    col_edge = col_bias.reshape(spec_dev, key_span // half_span, half_span)[:, :: qblocks + 1]
    bias_mid = jnp.where(band_mid[None], col_mid[:, None, None, :], masked_score)
    bias_edge = jnp.where(band_edge[None], col_edge[:, :, None, :], masked_score)
    row_limit = my_counts - first_bin
    encoded, pooled = band_attention(
        qkv, keyval_edges, bias_mid, bias_edge, enc_out, spectra, row_limit
    )
    spectra_all = lax.all_gather(pooled, "head", axis=0, tiled=True)
    local_width = mem_key.shape[1]
    memory_part = jnp.einsum(
        "spd,de->spe", rms_rows(spectra_all), mem_weights, preferred_element_type=jnp.float32
    ).astype(jnp.bfloat16)
    spec_count, part_len, part_width = memory_part.shape
    tok_count = token_ids.shape[1]
    id_cols = jnp.zeros((spec_count, part_len, 128), jnp.bfloat16)
    id_cols = id_cols.at[:, 0, :tok_count].set(token_ids.astype(jnp.bfloat16))
    payload = jnp.concatenate([memory_part, id_cols], axis=2)
    received = lax.all_to_all(payload, "seq", 0, 1, tiled=True)
    seq_count = lax.axis_size("seq")
    memory = received[:, :, :part_width]
    ids_one = received.reshape(seq_count, part_len, part_width + 128)[:, 0, part_width : part_width + tok_count]
    ids_one = ids_one.reshape(1, seq_count * tok_count).astype(jnp.int32)
    mem_len = memory.shape[1]
    bias_row = lax.dynamic_slice_in_dim(key_bias, seq_pos, 1, 0)
    pooled_bias = jnp.max(bias_row.reshape(1, mem_len, POOL), axis=2)
    count_row = lax.dynamic_slice_in_dim(valid_bins, seq_pos, 1, 0)
    mem_valid = jnp.arange(mem_len, dtype=jnp.int32)[None, :] * POOL < count_row[:, None]
    dec_width = embedding.shape[1]
    dec_head = dec_width // HD
    heads_here = local_width // dec_head
    share_width = dec_width // lax.axis_size("head")
    vocab = embedding.shape[0]
    onehot = (
        token_ids[:, :, None] == jnp.arange(vocab, dtype=jnp.int32)[None, None, :]
    ).astype(jnp.bfloat16)
    own_table = lax.dynamic_slice_in_dim(embedding, head_pos * share_width, share_width, 1)
    own_part = jnp.einsum(
        "stv,vd->std", onehot, own_table, preferred_element_type=jnp.float32
    ).astype(jnp.bfloat16)
    query_one = jnp.take(query_table, ids_one[0], axis=0)[None]
    mem_bias = jnp.where(mem_valid, pooled_bias, masked_score)[:, None, :]
    context_one = cross_attention(query_one, received, mem_bias, heads_here, dec_head)
    context_one = context_one.reshape(seq_count, tok_count, local_width)
    dec_context = lax.all_to_all(context_one, "seq", 0, 0, tiled=True)
    partial_sums = jnp.einsum(
        "ste,ed->std", dec_context, dec_out, preferred_element_type=jnp.float32
    )
    summed = lax.psum_scatter(
        partial_sums.astype(jnp.bfloat16), "head", scatter_dimension=2, tiled=True
    ).astype(jnp.float32)
    decoded = (own_part.astype(jnp.float32) + summed).astype(jnp.bfloat16)
    return (encoded, decoded)


def solution(mesh):
    return jax.shard_map(
        per_device,
        mesh=mesh,
        in_specs=(
            P("head", "seq", None),
            P(),
            P(),
            P(),
            P(),
            P(),
            P(),
            P(None, "seq"),
            P(),
            P(None, "head"),
            P(None, "head"),
            P(None, "head"),
            P("head", None),
        ),
        out_specs=(P("head", "seq", None), P(None, "seq", "head")),
        check_vma=False,
    )
```
